512 devices in a mesh: exp: 16 (over z), sky: 32 (over y, x, core).
Axes of the slice: x: 4, y: 4, z: 16, core: 2. Of those that a mesh axis runs over, the one named last changes fastest.
Arguments:
- sky_start: float32 [16, 128, 4096], P(None, None, 'sky'), may hold values from -6 to 6
- exposures: bfloat16 [16, 1024, 2, 128, 128], P('exp', 'sky'), may hold values from -16 to 16
- weights: bfloat16 [16, 1024, 2], P('exp', 'sky'), may hold values from 0.5 to 2
- footprint_owner: int32 [16, 1024, 1], P('exp', 'sky'), may hold values from 0 to 31; in each aligned block of 32 rows (0 to 31, 32 to 63, ..., all dimensions but the last counted through in order) at most 2 rows name the same one
- footprint_row: int32 [16, 1024], P('exp', 'sky'), may hold values from 0 to 15
- kernel_index: int32 [16, 1024, 2, 2], P('exp', 'sky'), may hold values from 0 to 7
- kernels: bfloat16 [8, 128, 128], replicated, may hold values from -1 to 1
Outputs:
- sky_image: float32 [16, 128, 4096], P(None, None, 'sky')
The draws below stay inside these ranges and needn't reach their ends.
Inputs may be any that keep to these rules, and one draw needn't show every extreme that they name: `footprint_owner`: the 32 footprint tiles of one device name one tile column at most 2 times, and some tile column exactly 2 times.
All inputs are finite; a program needn't handle non-finite values.
Results may differ from the reference program's by a relative error of at most 0.0035.
Values may be sent and summed in bfloat16 or wider, within the bound.
No kernel may reach another device: no remote copies, remote signals or barrier semaphores. Data moves between devices by JAX's collectives and lax.ppermute only.
A program may use at most 128 MiB of HBM per device.

```python
import math
import jax
import jax.numpy as jnp
import numpy as np
from jax import lax

TILE = 128
KERNELS = 8
EXPO = 2
SKY_ROWS = 16
ITERS = 2
FOOT_DEV = 32
FOOT_ROW = 1024
SKY_COLS = 4096
CAP = 2
N_EXP = 16
N_SKY = 32


def draw_kernels(key, part):
    key_diag, key_band, key_noise = jax.random.split(key, 3)
    row_ids = jnp.arange(TILE, dtype=jnp.int32)[:, None]
    col_ids = jnp.arange(TILE, dtype=jnp.int32)[None, :]
    offsets = (col_ids - row_ids).astype(jnp.float32)
    distance = jnp.abs(col_ids - row_ids)
    in_band = jnp.logical_and(distance >= 1, distance <= 10)
    profile = jnp.where(in_band, jnp.exp(-offsets * offsets / 50.0), 0.0)
    identity = jnp.eye(TILE, dtype=jnp.float32)
    diag_values = jax.random.uniform(key_diag, (KERNELS, TILE, 1), jnp.float32, 0.45, 0.65)
    band_values = jnp.clip(jax.random.normal(key_band, (KERNELS, TILE, TILE), jnp.float32), -3.0, 3.0)
    noise_values = jnp.clip(jax.random.normal(key_noise, (KERNELS, TILE, TILE), jnp.float32), -3.0, 3.0)
    kernel_set = diag_values * identity + 0.21 * profile * band_values
    kernel_set = kernel_set + 0.1 * noise_values / jnp.sqrt(float(TILE))
    return kernel_set.astype(jnp.bfloat16)


def set_ends(values, rng, smallest, top_value):
    place = [jax.random.randint(jax.random.fold_in(rng, axis), (), 0, length) for axis, length in enumerate(values.shape)]
    longest = values.shape.index(max(values.shape))
    beside = place[:longest] + [(place[longest] + 1) % values.shape[longest]] + place[longest + 1:]
    return values.at[tuple(place)].set(smallest).at[tuple(beside)].set(top_value)


def shard_levels(stream_key, dims, shards, smallest, largest):
    def one(position, blocks):
        steps = jax.random.uniform(jax.random.fold_in(jax.random.fold_in(stream_key, 6), position), (blocks,), jnp.float32, smallest / len(shards), largest / len(shards))
        return jnp.repeat(jnp.exp(steps), dims[position] // blocks).reshape((-1,) + (1,) * (len(dims) - position - 1))

    gain = one(*shards[0])
    for cut in shards[1:]:
        gain = gain * one(*cut)
    return gain


def routed_block(rng, own, number, rows, amount, top, bound, skew):
    sequence = jax.random.permutation(rng, amount)
    crowded, usual = portions_of(amount, rows * top, bound, skew, True), portions_of(amount, rows * top, bound, skew, False)
    places = jnp.arange(amount)

    def named(sizes, turn):
        used = int((sizes > 0).sum())
        fixed = max(1, used // 4)
        shifted = fixed + (places - fixed + turn * (used - fixed)) % max(1, amount - fixed)
        return jnp.zeros((amount,), jnp.int32).at[sequence[jnp.where(places < fixed, places, shifted)]].set(jnp.asarray(sizes, jnp.int32))

    sizes = jnp.where(number % 4 == 0, named(crowded, number // 4), named(usual, number - number // 4 - 1))
    mixed = jax.random.permutation(jax.random.fold_in(own, 3), amount)
    source_of, receiver = mixed[0:amount // 2 * 2:2], mixed[1:amount // 2 * 2:2]
    slack = jnp.minimum(sizes[source_of] - 1, bound - sizes[receiver]) // 2
    slack = jnp.where((source_of == sequence[0]) | (receiver == sequence[0]) | (sizes[receiver] == 0), 0, jnp.maximum(slack, 0))
    shifted = jax.random.randint(jax.random.fold_in(own, 4), (amount // 2,), 0, 1 << 20) % (slack + 1)
    sizes = sizes.at[source_of].add(-shifted).at[receiver].add(shifted)
    labels = jnp.searchsorted(jnp.cumsum(sizes), jnp.arange(rows * top), side="right").astype(jnp.int32)
    listing = labels.reshape(top, rows).T
    listing = listing[jax.random.permutation(jax.random.fold_in(own, 1), rows)]
    turn = jax.random.randint(jax.random.fold_in(own, 2), (rows, 1), 0, top)
    return jnp.take_along_axis(listing, (jnp.arange(top)[None, :] + turn) % top, axis=1)


def portions_of(number_of, total, bound, lean, full):
    portions = [(1 << 20) // math.isqrt(standing ** lean) + 1 for standing in range(1, number_of + 1)]
    largest = bound if full else min(bound, max(-(-total // number_of), total * portions[0] // sum(portions)))
    least = 1 if total - largest >= number_of - 1 else 0
    given, surplus = [largest] + [least] * (number_of - 1), total - largest - least * (number_of - 1)
    while surplus > 0:
        movable = [i for i in range(1, number_of) if given[i] < largest] or [i for i in range(1, number_of) if given[i] < bound]
        whole, remaining = sum([portions[i] for i in movable]), surplus
        for i in movable:
            addition = min(bound - given[i], max(1, remaining * portions[i] // whole), surplus)
            given[i] = given[i] + addition
            surplus = surplus - addition
    return np.array(given)


def scatter_about(own_key, dims, scale, most, pieces=(), kind=jnp.bfloat16):
    loudness = shard_levels(own_key, dims, pieces, -0.22, 0.18) if pieces else 1.0
    array = jax.random.normal(own_key, dims, jnp.float32) * scale * loudness
    return jnp.minimum(jnp.maximum(array, -most), most).astype(kind)


def setup_inputs(seed: int = 0) -> dict:
    arg_keys = jax.random.split(jax.random.key(seed), 8)
    sky_start = scatter_about(arg_keys[0], (SKY_ROWS, TILE, SKY_COLS), 1.0, 6.0, ((2, 32),), jnp.float32)
    exposures = scatter_about(arg_keys[1], (N_EXP, FOOT_ROW, EXPO, TILE, TILE), 4.0, 16.0, ((0, 16), (1, 32)))
    weights = jnp.clip(jnp.exp(math.log(2.0) - 1.3862944 * jax.random.uniform(arg_keys[2], (N_EXP, FOOT_ROW, EXPO), jnp.float32) ** shard_levels(arg_keys[2], (N_EXP, FOOT_ROW, EXPO), ((0, 16), (1, 32)), -0.2, 0.2)), 0.5, 2.0).astype(jnp.bfloat16)
    footprint_owner_keys = jax.random.split(jax.random.fold_in(arg_keys[3], 1), N_EXP * FOOT_ROW // FOOT_DEV)
    footprint_owner_turns = jax.random.permutation(jax.random.fold_in(arg_keys[3], 3), N_EXP * FOOT_ROW // FOOT_DEV)
    footprint_owner = jax.vmap(lambda own, number: routed_block(jax.random.fold_in(arg_keys[3], 2), own, number, FOOT_DEV, N_SKY, 1, CAP, 2))(footprint_owner_keys, footprint_owner_turns).reshape((N_EXP, FOOT_ROW, 1))
    footprint_row = set_ends(jax.random.randint(arg_keys[4], (N_EXP, FOOT_ROW), 0, SKY_ROWS), jax.random.fold_in(arg_keys[4], 1), 0, SKY_ROWS - 1).astype(jnp.int32)
    kernel_index = set_ends(jax.random.randint(arg_keys[5], (N_EXP, FOOT_ROW, EXPO, 2), 0, KERNELS), jax.random.fold_in(arg_keys[5], 1), 0, KERNELS - 1).astype(jnp.int32)
    kernels = draw_kernels(jax.random.fold_in(arg_keys[7], 71), 0)
    return dict(sky_start=sky_start, exposures=exposures, weights=weights, footprint_owner=footprint_owner, footprint_row=footprint_row, kernel_index=kernel_index, kernels=kernels)


weight_ceiling = 2.0


def adjoint_tiles(fetched, left_kernels, right_kernels, tile_weights, observed):
    left_product = jnp.einsum('fetu,fuv->fetv', left_kernels, fetched)
    left_product = lax.optimization_barrier(left_product.astype(jnp.bfloat16)).astype(jnp.float32)
    predicted = jnp.einsum('fetv,fewv->fetw', left_product, right_kernels)
    residual = tile_weights.astype(jnp.float32)[..., None, None] * (predicted - observed.astype(jnp.float32))
    residual = lax.optimization_barrier(residual.astype(jnp.bfloat16)).astype(jnp.float32)
    back_product = jnp.einsum('feut,feuw->fetw', left_kernels, residual)
    back_product = lax.optimization_barrier(back_product.astype(jnp.bfloat16)).astype(jnp.float32)
    summed = jnp.sum(jnp.einsum('fetw,fewv->fetv', back_product, right_kernels), axis=1)
    return summed.astype(jnp.bfloat16)


def reference(sky_start, exposures, weights, footprint_owner, footprint_row, kernel_index, kernels):
    tile_ids = (footprint_row * N_SKY + footprint_owner[..., 0]).astype(jnp.int32).reshape(-1, FOOT_DEV)
    hits = jnp.zeros((SKY_ROWS * N_SKY,), jnp.float32).at[tile_ids.reshape(-1)].add(1.0)
    counts = EXPO * hits
    kernel_wide = kernels.astype(jnp.float32)
    blocks = (tile_ids,
              exposures.reshape(-1, FOOT_DEV, EXPO, TILE, TILE),
              weights.reshape(-1, FOOT_DEV, EXPO),
              kernel_index.reshape(-1, FOOT_DEV, EXPO, 2))
    prior_weight = N_EXP * FOOT_DEV * EXPO / (8.0 * SKY_ROWS)
    count_image = jnp.repeat(counts.reshape(SKY_ROWS, 1, N_SKY), TILE, axis=2)
    sky_now = sky_start
    for iteration in range(ITERS):
        sky_tiles = sky_now.reshape(SKY_ROWS, TILE, N_SKY, TILE).transpose(0, 2, 1, 3).reshape(-1, TILE, TILE)
        sky_tiles = lax.optimization_barrier(sky_tiles.astype(jnp.bfloat16)).astype(jnp.float32)

        def block_step(accumulated, block_items):
            tile_block, observed, tile_weights, kernel_ids = block_items
            fetched = sky_tiles[tile_block]
            adjoint = adjoint_tiles(fetched, kernel_wide[kernel_ids[..., 0]], kernel_wide[kernel_ids[..., 1]],
                                    tile_weights, observed)
            return accumulated.at[tile_block].add(adjoint.astype(jnp.float32)), None

        total, unused = lax.scan(block_step, jnp.zeros((SKY_ROWS * N_SKY, TILE, TILE), jnp.float32), blocks)
        total_image = total.reshape(SKY_ROWS, N_SKY, TILE, TILE).transpose(0, 2, 1, 3).reshape(SKY_ROWS, TILE, N_SKY * TILE)
        image_rows = sky_now.reshape(SKY_ROWS * TILE, N_SKY * TILE)
        padded = jnp.pad(image_rows, 1)
        laplacian = 4.0 * image_rows - padded[:-2, 1:-1] - padded[2:, 1:-1] - padded[1:-1, :-2] - padded[1:-1, 2:]
        laplacian = laplacian.reshape(SKY_ROWS, TILE, N_SKY * TILE)
        sky_now = sky_now - (total_image + prior_weight * laplacian) / (weight_ceiling * count_image + 8.0 * prior_weight)
    return sky_now
```

```python
import jax
import jax.numpy as jnp
from jax import lax
from jax.sharding import PartitionSpec as P

ITERS = 2


weight_ceiling = 2.0


def padded_2(cells, sides, width):
    for axis, dim in sides:
        count = lax.axis_size(axis)
        ends = count - 1
        head = lax.slice_in_dim(cells, 0, width, axis=dim)
        tail = lax.slice_in_dim(cells, cells.shape[dim] - width, cells.shape[dim], axis=dim)
        cells = jnp.concatenate(
            [
                lax.ppermute(tail, axis, [(i, (i + 1) % count) for i in range(ends)]),
                cells,
                lax.ppermute(head, axis, [((i + 1) % count, i) for i in range(ends)]),
            ],
            axis=dim,
        )
    return cells


def pick_kernels(kernel_ids, kernels):
    table_size = kernels.shape[0]
    tile_edge = kernels.shape[1]
    onehot = (kernel_ids[..., None] == jnp.arange(table_size, dtype=jnp.int32)).astype(jnp.bfloat16)
    onehot = onehot.reshape(-1, table_size)
    selected = jnp.dot(onehot, kernels.reshape(table_size, -1), preferred_element_type=jnp.float32)
    selected = selected.astype(jnp.bfloat16).reshape(kernel_ids.shape + (tile_edge, tile_edge))
    return (selected[..., 0, :, :], selected[..., 1, :, :])


def adjoint_tiles(fetched, left_kernels, right_kernels, tile_weights, observed):
    left_product = jnp.einsum(
        "fetu,fuv->fetv", left_kernels, fetched, preferred_element_type=jnp.float32
    ).astype(jnp.bfloat16)
    predicted = jnp.einsum(
        "fetv,fewv->fetw", left_product, right_kernels, preferred_element_type=jnp.float32
    )
    residual = tile_weights.astype(jnp.float32)[..., None, None] * (
        predicted - observed.astype(jnp.float32)
    )
    residual = residual.astype(jnp.bfloat16)
    back_product = jnp.einsum(
        "feut,feuw->fetw", left_kernels, residual, preferred_element_type=jnp.float32
    ).astype(jnp.bfloat16)
    summed = jnp.sum(
        jnp.einsum(
            "fetw,fewv->fetv", back_product, right_kernels, preferred_element_type=jnp.float32
        ),
        axis=1,
    )
    return summed.astype(jnp.bfloat16)


def laplace_image(padded):
    image_rows = padded.reshape(padded.shape[0] * padded.shape[1], padded.shape[2])
    center = image_rows[:, 1:-1]
    vertical = jnp.pad(center, ((1, 1), (0, 0)))
    laplacian = 4.0 * center - image_rows[:, :-2] - image_rows[:, 2:] - vertical[:-2] - vertical[2:]
    return laplacian.reshape(padded.shape[0], padded.shape[1], padded.shape[2] - 2)


def per_device(
    sky_start, exposures, weights, footprint_owner, footprint_row, kernel_index, kernels
):
    sky_rows = sky_start.shape[0]
    tile_edge = sky_start.shape[1]
    foot_tiles = footprint_row.shape[1]
    expo_count = exposures.shape[2]
    n_sky = lax.axis_size("sky")
    n_exp = lax.axis_size("exp")
    capacity = max(2, 3 * foot_tiles // (2 * n_sky))
    slot_count = n_sky * capacity
    prior_weight = n_exp * foot_tiles * expo_count / (8.0 * sky_rows)
    owner_ids = footprint_owner[0, :, 0]
    tile_rows = footprint_row[0]
    onehot_owner = (owner_ids[:, None] == jnp.arange(n_sky, dtype=jnp.int32)[None, :]).astype(
        jnp.int32
    )
    ranks = jnp.sum((jnp.cumsum(onehot_owner, axis=0) - onehot_owner) * onehot_owner, axis=1)
    slot_of = owner_ids * capacity + ranks
    packing = jnp.arange(slot_count, dtype=jnp.int32)[:, None] == slot_of[None, :]
    packing_half = packing.astype(jnp.bfloat16)
    requested = jnp.sum(jnp.where(packing, tile_rows[None, :] + 1, 0), axis=1) - 1
    observed = exposures[0]
    tile_weights = weights[0]
    kernel_ids = kernel_index[0]
    incoming = lax.all_to_all(requested, "sky", split_axis=0, concat_axis=0, tiled=True)
    left_kernels, right_kernels = pick_kernels(kernel_ids, kernels)
    receive_map = jnp.arange(sky_rows, dtype=jnp.int32)[:, None] == incoming[None, :]
    local_counts = float(expo_count) * jnp.sum(receive_map.astype(jnp.float32), axis=1)
    counts = jnp.sum(lax.all_gather(local_counts, "exp", axis=0), axis=0)
    receive_half = receive_map.astype(jnp.bfloat16)
    safe_rows = jnp.maximum(incoming, 0)
    rows_per = sky_rows // n_exp
    own_rows = lax.axis_index("exp") * rows_per
    own_counts = lax.dynamic_slice_in_dim(counts, own_rows, rows_per)
    denominator = weight_ceiling * own_counts[:, None, None] + 8.0 * prior_weight
    sky_now = sky_start
    for iteration in range(ITERS):
        sky_half = sky_now.astype(jnp.bfloat16)
        replies = lax.all_to_all(
            sky_half[safe_rows], "sky", split_axis=0, concat_axis=0, tiled=True
        )
        fetched = replies[slot_of]
        adjoint = adjoint_tiles(fetched, left_kernels, right_kernels, tile_weights, observed)
        outgoing = jnp.dot(
            packing_half, adjoint.reshape(foot_tiles, -1), preferred_element_type=jnp.float32
        )
        arrived = lax.all_to_all(
            outgoing.astype(jnp.bfloat16), "sky", split_axis=0, concat_axis=0, tiled=True
        )
        partial_value = jnp.dot(receive_half, arrived, preferred_element_type=jnp.float32).reshape(
            sky_rows, tile_edge, tile_edge
        )
        row_parts = lax.all_to_all(
            partial_value.astype(jnp.bfloat16), "exp", split_axis=0, concat_axis=0, tiled=True
        )
        summed = jnp.sum(
            row_parts.astype(jnp.float32).reshape(n_exp, rows_per, tile_edge, tile_edge), axis=0
        )
        laplacian = laplace_image(padded_2(sky_now, (("sky", 2),), 1))
        own_laplacian = lax.dynamic_slice_in_dim(laplacian, own_rows, rows_per)
        step = (summed + prior_weight * own_laplacian) / denominator
        steps = lax.all_gather(step.astype(jnp.bfloat16), "exp", axis=0, tiled=True)
        sky_now = sky_now - steps.astype(jnp.float32)
    return sky_now


def solution(mesh):
    in_specs = (
        P(None, None, "sky"),
        P("exp", "sky", None, None, None),
        P("exp", "sky", None),
        P("exp", "sky", None),
        P("exp", "sky"),
        P("exp", "sky", None, None),
        P(),
    )
    out_specs = P(None, None, "sky")
    return jax.shard_map(
        per_device, mesh=mesh, in_specs=in_specs, out_specs=out_specs, check_vma=False
    )
```

```python
import jax
import jax.numpy as jnp
from jax import lax
from jax.sharding import PartitionSpec as P

ITERS = 2


weight_ceiling = 2.0


def padded_2(cells, sides, width):
    for axis, dim in sides:
        count = lax.axis_size(axis)
        ends = count - 1
        head = lax.slice_in_dim(cells, 0, width, axis=dim)
        tail = lax.slice_in_dim(cells, cells.shape[dim] - width, cells.shape[dim], axis=dim)
        cells = jnp.concatenate(
            [
                lax.ppermute(tail, axis, [(i, (i + 1) % count) for i in range(ends)]),
                cells,
                lax.ppermute(head, axis, [((i + 1) % count, i) for i in range(ends)]),
            ],
            axis=dim,
        )
    return cells


def pick_kernels(kernel_ids, kernels):
    table_size = kernels.shape[0]
    tile_edge = kernels.shape[1]
    onehot = (kernel_ids[..., None] == jnp.arange(table_size, dtype=jnp.int32)).astype(jnp.bfloat16)
    onehot = onehot.reshape(-1, table_size)
    selected = jnp.dot(onehot, kernels.reshape(table_size, -1), preferred_element_type=jnp.float32)
    selected = selected.astype(jnp.bfloat16).reshape(kernel_ids.shape + (tile_edge, tile_edge))
    return (selected[..., 0, :, :], selected[..., 1, :, :])


def adjoint_tiles(fetched, left_kernels, right_kernels, tile_weights, observed):
    left_product = jnp.einsum(
        "fetu,fuv->fetv", left_kernels, fetched, preferred_element_type=jnp.float32
    ).astype(jnp.bfloat16)
    predicted = jnp.einsum(
        "fetv,fewv->fetw", left_product, right_kernels, preferred_element_type=jnp.float32
    )
    residual = tile_weights.astype(jnp.float32)[..., None, None] * (
        predicted - observed.astype(jnp.float32)
    )
    residual = residual.astype(jnp.bfloat16)
    back_product = jnp.einsum(
        "feut,feuw->fetw", left_kernels, residual, preferred_element_type=jnp.float32
    ).astype(jnp.bfloat16)
    summed = jnp.sum(
        jnp.einsum(
            "fetw,fewv->fetv", back_product, right_kernels, preferred_element_type=jnp.float32
        ),
        axis=1,
    )
    return summed.astype(jnp.bfloat16)


def laplace_image(padded):
    image_rows = padded.reshape(padded.shape[0] * padded.shape[1], padded.shape[2])
    center = image_rows[:, 1:-1]
    vertical = jnp.pad(center, ((1, 1), (0, 0)))
    laplacian = 4.0 * center - image_rows[:, :-2] - image_rows[:, 2:] - vertical[:-2] - vertical[2:]
    return laplacian.reshape(padded.shape[0], padded.shape[1], padded.shape[2] - 2)


def per_device(
    sky_start, exposures, weights, footprint_owner, footprint_row, kernel_index, kernels
):
    sky_rows = sky_start.shape[0]
    tile_edge = sky_start.shape[1]
    foot_tiles = footprint_row.shape[1]
    expo_count = exposures.shape[2]
    n_sky = lax.axis_size("sky")
    n_exp = lax.axis_size("exp")
    capacity = max(2, 3 * foot_tiles // (2 * n_sky))
    slot_count = n_sky * capacity
    prior_weight = n_exp * foot_tiles * expo_count / (8.0 * sky_rows)
    owner_ids = footprint_owner[0, :, 0]
    tile_rows = footprint_row[0]
    onehot_owner = (owner_ids[:, None] == jnp.arange(n_sky, dtype=jnp.int32)[None, :]).astype(
        jnp.int32
    )
    ranks = jnp.sum((jnp.cumsum(onehot_owner, axis=0) - onehot_owner) * onehot_owner, axis=1)
    slot_of = owner_ids * capacity + ranks
    packing = jnp.arange(slot_count, dtype=jnp.int32)[:, None] == slot_of[None, :]
    packing_half = packing.astype(jnp.bfloat16)
    requested = jnp.sum(jnp.where(packing, tile_rows[None, :] + 1, 0), axis=1) - 1
    observed = exposures[0]
    tile_weights = weights[0]
    kernel_ids = kernel_index[0]
    incoming = lax.all_to_all(requested, "sky", split_axis=0, concat_axis=0, tiled=True)
    left_kernels, right_kernels = pick_kernels(kernel_ids, kernels)
    receive_map = jnp.arange(sky_rows, dtype=jnp.int32)[:, None] == incoming[None, :]
    local_counts = float(expo_count) * jnp.sum(receive_map.astype(jnp.float32), axis=1)
    receive_half = receive_map.astype(jnp.bfloat16)
    safe_rows = jnp.maximum(incoming, 0)
    rows_per = sky_rows // n_exp
    own_rows = lax.axis_index("exp") * rows_per
    count_block = jnp.broadcast_to(
        local_counts.astype(jnp.bfloat16)[None, :, None], (n_exp, sky_rows, tile_edge)
    )
    sky_now = sky_start
    for iteration in range(ITERS):
        sky_half = sky_now.astype(jnp.bfloat16)
        replies = lax.all_to_all(
            sky_half[safe_rows], "sky", split_axis=0, concat_axis=0, tiled=True
        )
        fetched = replies[slot_of]
        adjoint = adjoint_tiles(fetched, left_kernels, right_kernels, tile_weights, observed)
        outgoing = jnp.dot(
            packing_half, adjoint.reshape(foot_tiles, -1), preferred_element_type=jnp.float32
        )
        arrived = lax.all_to_all(
            outgoing.astype(jnp.bfloat16), "sky", split_axis=0, concat_axis=0, tiled=True
        )
        partial_value = jnp.dot(receive_half, arrived, preferred_element_type=jnp.float32)
        payload = partial_value.astype(jnp.bfloat16).reshape(n_exp, rows_per * tile_edge, tile_edge)
        if iteration == 0:
            payload = jnp.concatenate([payload, count_block], axis=1)
        row_parts = lax.all_to_all(payload, "exp", split_axis=0, concat_axis=0, tiled=True)
        summed = jnp.sum(row_parts.astype(jnp.float32).reshape((n_exp,) + payload.shape[1:]), axis=0)
        if iteration == 0:
            counts = summed[rows_per * tile_edge :, 0]
            denominator = weight_ceiling * counts + 8.0 * prior_weight
            own_denominator = lax.dynamic_slice_in_dim(denominator, own_rows, rows_per)
        own_total = summed[: rows_per * tile_edge].reshape(rows_per, tile_edge, tile_edge)
        scaled = own_total / own_denominator[:, None, None]
        gathered = lax.all_gather(scaled.astype(jnp.bfloat16), "exp", axis=0, tiled=True)
        laplacian = laplace_image(padded_2(sky_now, (("sky", 2),), 1))
        smooth = prior_weight * laplacian / denominator[:, None, None]
        sky_now = sky_now - (gathered.astype(jnp.float32) + smooth)
    return sky_now


def solution(mesh):
    in_specs = (
        P(None, None, "sky"),
        P("exp", "sky", None, None, None),
        P("exp", "sky", None),
        P("exp", "sky", None),
        P("exp", "sky"),
        P("exp", "sky", None, None),
        P(),
    )
    out_specs = P(None, None, "sky")
    return jax.shard_map(
        per_device, mesh=mesh, in_specs=in_specs, out_specs=out_specs, check_vma=False
    )
```

```python
import jax
import jax.numpy as jnp
from jax import lax
from jax.sharding import PartitionSpec as P

ITERS = 2


weight_ceiling = 2.0


def padded_2(cells, sides, width):
    for axis, dim in sides:
        count = lax.axis_size(axis)
        ends = count - 1
        head = lax.slice_in_dim(cells, 0, width, axis=dim)
        tail = lax.slice_in_dim(cells, cells.shape[dim] - width, cells.shape[dim], axis=dim)
        cells = jnp.concatenate(
            [
                lax.ppermute(tail, axis, [(i, (i + 1) % count) for i in range(ends)]),
                cells,
                lax.ppermute(head, axis, [((i + 1) % count, i) for i in range(ends)]),
            ],
            axis=dim,
        )
    return cells


def pick_kernels(kernel_ids, kernels):
    table_size = kernels.shape[0]
    tile_edge = kernels.shape[1]
    onehot = (kernel_ids[..., None] == jnp.arange(table_size, dtype=jnp.int32)).astype(jnp.bfloat16)
    onehot = onehot.reshape(-1, table_size)
    selected = jnp.dot(onehot, kernels.reshape(table_size, -1), preferred_element_type=jnp.float32)
    selected = selected.astype(jnp.bfloat16).reshape(kernel_ids.shape + (tile_edge, tile_edge))
    return (selected[..., 0, :, :], selected[..., 1, :, :])


def adjoint_tiles(fetched, left_kernels, right_kernels, tile_weights, observed):
    left_product = jnp.einsum(
        "fetu,fuv->fetv", left_kernels, fetched, preferred_element_type=jnp.float32
    ).astype(jnp.bfloat16)
    predicted = jnp.einsum(
        "fetv,fewv->fetw", left_product, right_kernels, preferred_element_type=jnp.float32
    )
    residual = tile_weights.astype(jnp.float32)[..., None, None] * (
        predicted - observed.astype(jnp.float32)
    )
    residual = residual.astype(jnp.bfloat16)
    back_product = jnp.einsum(
        "feut,feuw->fetw", left_kernels, residual, preferred_element_type=jnp.float32
    ).astype(jnp.bfloat16)
    summed = jnp.sum(
        jnp.einsum(
            "fetw,fewv->fetv", back_product, right_kernels, preferred_element_type=jnp.float32
        ),
        axis=1,
    )
    return summed.astype(jnp.bfloat16)


def laplace_image(padded):
    image_rows = padded.reshape(padded.shape[0] * padded.shape[1], padded.shape[2])
    center = image_rows[:, 1:-1]
    vertical = jnp.pad(center, ((1, 1), (0, 0)))
    laplacian = 4.0 * center - image_rows[:, :-2] - image_rows[:, 2:] - vertical[:-2] - vertical[2:]
    return laplacian.reshape(padded.shape[0], padded.shape[1], padded.shape[2] - 2)


def per_device(
    sky_start, exposures, weights, footprint_owner, footprint_row, kernel_index, kernels
):
    sky_rows = sky_start.shape[0]
    tile_edge = sky_start.shape[1]
    foot_tiles = footprint_row.shape[1]
    expo_count = exposures.shape[2]
    n_sky = lax.axis_size("sky")
    n_exp = lax.axis_size("exp")
    capacity = max(2, 3 * foot_tiles // (2 * n_sky))
    slot_count = n_sky * capacity
    prior_weight = n_exp * foot_tiles * expo_count / (8.0 * sky_rows)
    owner_ids = footprint_owner[0, :, 0]
    tile_rows = footprint_row[0]
    onehot_owner = (owner_ids[:, None] == jnp.arange(n_sky, dtype=jnp.int32)[None, :]).astype(
        jnp.int32
    )
    ranks = jnp.sum((jnp.cumsum(onehot_owner, axis=0) - onehot_owner) * onehot_owner, axis=1)
    slot_of = owner_ids * capacity + ranks
    packing = jnp.arange(slot_count, dtype=jnp.int32)[:, None] == slot_of[None, :]
    requested = jnp.sum(jnp.where(packing, tile_rows[None, :] + 1, 0), axis=1) - 1
    slot_source = jnp.sum(jnp.where(packing, jnp.arange(foot_tiles)[None, :] + 1, 0), axis=1) - 1
    slot_source = jnp.where(slot_source < 0, foot_tiles, slot_source)
    observed = exposures[0]
    tile_weights = weights[0]
    kernel_ids = kernel_index[0]
    incoming = lax.all_to_all(requested, "sky", split_axis=0, concat_axis=0, tiled=True)
    left_kernels, right_kernels = pick_kernels(kernel_ids, kernels)
    receive_map = jnp.arange(sky_rows, dtype=jnp.int32)[:, None] == incoming[None, :]
    local_counts = float(expo_count) * jnp.sum(receive_map.astype(jnp.float32), axis=1)
    receive_half = receive_map.astype(jnp.bfloat16)
    safe_rows = jnp.maximum(incoming, 0)
    rows_per = sky_rows // n_exp
    own_rows = lax.axis_index("exp") * rows_per
    count_block = jnp.broadcast_to(
        local_counts.astype(jnp.bfloat16)[None, :, None], (n_exp, sky_rows, tile_edge)
    )
    sky_now = sky_start
    for iteration in range(ITERS):
        sky_half = sky_now.astype(jnp.bfloat16)
        replies = lax.all_to_all(
            sky_half[safe_rows], "sky", split_axis=0, concat_axis=0, tiled=True
        )
        fetched = replies[slot_of]
        adjoint = adjoint_tiles(fetched, left_kernels, right_kernels, tile_weights, observed)
        padded_adjoint = jnp.concatenate(
            [adjoint, jnp.zeros((1, tile_edge, tile_edge), adjoint.dtype)], axis=0
        )
        outgoing = padded_adjoint[slot_source]
        arrived = lax.all_to_all(outgoing, "sky", split_axis=0, concat_axis=0, tiled=True)
        partial_value = jnp.einsum(
            "rj,juv->ruv", receive_half, arrived, preferred_element_type=jnp.float32
        )
        payload = partial_value.astype(jnp.bfloat16).reshape(n_exp, rows_per * tile_edge, tile_edge)
        if iteration == 0:
            payload = jnp.concatenate([payload, count_block], axis=1)
        row_parts = lax.all_to_all(payload, "exp", split_axis=0, concat_axis=0, tiled=True)
        summed = jnp.sum(row_parts.astype(jnp.float32).reshape((n_exp,) + payload.shape[1:]), axis=0)
        if iteration == 0:
            counts = summed[rows_per * tile_edge :, 0]
            denominator = weight_ceiling * counts + 8.0 * prior_weight
            own_denominator = lax.dynamic_slice_in_dim(denominator, own_rows, rows_per)
        own_total = summed[: rows_per * tile_edge].reshape(rows_per, tile_edge, tile_edge)
        scaled = own_total / own_denominator[:, None, None]
        gathered = lax.all_gather(scaled.astype(jnp.bfloat16), "exp", axis=0, tiled=True)
        laplacian = laplace_image(padded_2(sky_now, (("sky", 2),), 1))
        smooth = prior_weight * laplacian / denominator[:, None, None]
        sky_now = sky_now - (gathered.astype(jnp.float32) + smooth)
    return sky_now


def solution(mesh):
    in_specs = (
        P(None, None, "sky"),
        P("exp", "sky", None, None, None),
        P("exp", "sky", None),
        P("exp", "sky", None),
        P("exp", "sky"),
        P("exp", "sky", None, None),
        P(),
    )
    out_specs = P(None, None, "sky")
    return jax.shard_map(
        per_device, mesh=mesh, in_specs=in_specs, out_specs=out_specs, check_vma=False
    )
```

```python
import jax
import jax.numpy as jnp
from jax import lax
from jax.sharding import PartitionSpec as P

ITERS = 2


weight_ceiling = 2.0


def padded_2(cells, sides, width):
    for axis, dim in sides:
        count = lax.axis_size(axis)
        ends = count - 1
        head = lax.slice_in_dim(cells, 0, width, axis=dim)
        tail = lax.slice_in_dim(cells, cells.shape[dim] - width, cells.shape[dim], axis=dim)
        cells = jnp.concatenate(
            [
                lax.ppermute(tail, axis, [(i, (i + 1) % count) for i in range(ends)]),
                cells,
                lax.ppermute(head, axis, [((i + 1) % count, i) for i in range(ends)]),
            ],
            axis=dim,
        )
    return cells


def pick_kernels(kernel_ids, kernels):
    table_size = kernels.shape[0]
    tile_edge = kernels.shape[1]
    onehot = (kernel_ids[..., None] == jnp.arange(table_size, dtype=jnp.int32)).astype(jnp.bfloat16)
    onehot = onehot.reshape(-1, table_size)
    selected = jnp.dot(onehot, kernels.reshape(table_size, -1), preferred_element_type=jnp.float32)
    selected = selected.astype(jnp.bfloat16).reshape(kernel_ids.shape + (tile_edge, tile_edge))
    return (selected[..., 0, :, :], selected[..., 1, :, :])


def adjoint_tiles(fetched, left_kernels, right_kernels, tile_weights, observed):
    left_product = jnp.einsum(
        "fetu,fuv->fetv", left_kernels, fetched, preferred_element_type=jnp.float32
    ).astype(jnp.bfloat16)
    predicted = jnp.einsum(
        "fetv,fewv->fetw", left_product, right_kernels, preferred_element_type=jnp.float32
    )
    residual = tile_weights.astype(jnp.float32)[..., None, None] * (
        predicted - observed.astype(jnp.float32)
    )
    residual = residual.astype(jnp.bfloat16)
    back_product = jnp.einsum(
        "feut,feuw->fetw", left_kernels, residual, preferred_element_type=jnp.float32
    ).astype(jnp.bfloat16)
    summed = jnp.sum(
        jnp.einsum(
            "fetw,fewv->fetv", back_product, right_kernels, preferred_element_type=jnp.float32
        ),
        axis=1,
    )
    return summed.astype(jnp.bfloat16)


def laplace_image(padded):
    image_rows = padded.reshape(padded.shape[0] * padded.shape[1], padded.shape[2])
    center = image_rows[:, 1:-1]
    vertical = jnp.pad(center, ((1, 1), (0, 0)))
    laplacian = 4.0 * center - image_rows[:, :-2] - image_rows[:, 2:] - vertical[:-2] - vertical[2:]
    return laplacian.reshape(padded.shape[0], padded.shape[1], padded.shape[2] - 2)


def per_device(
    sky_start, exposures, weights, footprint_owner, footprint_row, kernel_index, kernels
):
    sky_rows = sky_start.shape[0]
    tile_edge = sky_start.shape[1]
    foot_tiles = footprint_row.shape[1]
    expo_count = exposures.shape[2]
    n_sky = lax.axis_size("sky")
    n_exp = lax.axis_size("exp")
    capacity = max(2, 3 * foot_tiles // (2 * n_sky))
    slot_count = n_sky * capacity
    prior_weight = n_exp * foot_tiles * expo_count / (8.0 * sky_rows)
    owner_ids = footprint_owner[0, :, 0]
    tile_rows = footprint_row[0]
    onehot_owner = (owner_ids[:, None] == jnp.arange(n_sky, dtype=jnp.int32)[None, :]).astype(
        jnp.int32
    )
    ranks = jnp.sum((jnp.cumsum(onehot_owner, axis=0) - onehot_owner) * onehot_owner, axis=1)
    slot_of = owner_ids * capacity + ranks
    packing = jnp.arange(slot_count, dtype=jnp.int32)[:, None] == slot_of[None, :]
    requested = jnp.sum(jnp.where(packing, tile_rows[None, :] + 1, 0), axis=1) - 1
    slot_source = jnp.sum(jnp.where(packing, jnp.arange(foot_tiles)[None, :] + 1, 0), axis=1) - 1
    slot_source = jnp.where(slot_source < 0, foot_tiles, slot_source)
    observed = exposures[0]
    tile_weights = weights[0]
    kernel_ids = kernel_index[0]
    incoming = lax.all_to_all(requested, "sky", split_axis=0, concat_axis=0, tiled=True)
    left_kernels, right_kernels = pick_kernels(kernel_ids, kernels)
    receive_map = jnp.arange(sky_rows, dtype=jnp.int32)[:, None] == incoming[None, :]
    local_counts = float(expo_count) * jnp.sum(receive_map.astype(jnp.float32), axis=1)
    receive_half = receive_map.astype(jnp.bfloat16)
    safe_rows = jnp.maximum(incoming, 0)
    rows_per = sky_rows // n_exp
    own_rows = lax.axis_index("exp") * rows_per
    count_block = jnp.broadcast_to(
        local_counts.astype(jnp.bfloat16)[None, :, None], (n_exp, sky_rows, tile_edge)
    )
    sky_now = sky_start
    for iteration in range(ITERS):
        sky_half = sky_now.astype(jnp.bfloat16)
        replies = lax.all_to_all(
            sky_half[safe_rows], "sky", split_axis=0, concat_axis=0, tiled=True
        )
        fetched = replies[slot_of]
        adjoint = adjoint_tiles(fetched, left_kernels, right_kernels, tile_weights, observed)
        padded_adjoint = jnp.concatenate(
            [adjoint, jnp.zeros((1, tile_edge, tile_edge), adjoint.dtype)], axis=0
        )
        outgoing = padded_adjoint[slot_source]
        arrived = lax.all_to_all(outgoing, "sky", split_axis=0, concat_axis=0, tiled=True)
        partial_value = jnp.einsum(
            "rj,juv->ruv", receive_half, arrived, preferred_element_type=jnp.float32
        )
        payload = partial_value.astype(jnp.bfloat16).reshape(n_exp, rows_per * tile_edge, tile_edge)
        if iteration == 0:
            payload = jnp.concatenate([payload, count_block], axis=1)
        row_parts = lax.all_to_all(payload, "exp", split_axis=0, concat_axis=0, tiled=True)
        summed = jnp.sum(row_parts.astype(jnp.float32).reshape((n_exp,) + payload.shape[1:]), axis=0)
        if iteration == 0:
            counts = summed[rows_per * tile_edge :, 0]
            denominator = weight_ceiling * counts + 8.0 * prior_weight
            own_denominator = lax.dynamic_slice_in_dim(denominator, own_rows, rows_per)
        own_total = summed[: rows_per * tile_edge].reshape(rows_per, tile_edge, tile_edge)
        scaled = own_total / own_denominator[:, None, None]
        gathered = lax.all_to_all(
            jnp.broadcast_to(scaled.astype(jnp.bfloat16)[None], (n_exp,) + scaled.shape).reshape(
                sky_rows, tile_edge, tile_edge
            ),
            "exp",
            split_axis=0,
            concat_axis=0,
            tiled=True,
        )
        laplacian = laplace_image(padded_2(sky_now, (("sky", 2),), 1))
        smooth = prior_weight * laplacian / denominator[:, None, None]
        sky_now = sky_now - (gathered.astype(jnp.float32) + smooth)
    return sky_now


def solution(mesh):
    in_specs = (
        P(None, None, "sky"),
        P("exp", "sky", None, None, None),
        P("exp", "sky", None),
        P("exp", "sky", None),
        P("exp", "sky"),
        P("exp", "sky", None, None),
        P(),
    )
    out_specs = P(None, None, "sky")
    return jax.shard_map(
        per_device, mesh=mesh, in_specs=in_specs, out_specs=out_specs, check_vma=False
    )
```

```python
import jax
import jax.numpy as jnp
from jax import lax
from jax.sharding import PartitionSpec as P

ITERS = 2


weight_ceiling = 2.0


def padded_2(cells, sides, width):
    for axis, dim in sides:
        count = lax.axis_size(axis)
        ends = count - 1
        head = lax.slice_in_dim(cells, 0, width, axis=dim)
        tail = lax.slice_in_dim(cells, cells.shape[dim] - width, cells.shape[dim], axis=dim)
        cells = jnp.concatenate(
            [
                lax.ppermute(tail, axis, [(i, (i + 1) % count) for i in range(ends)]),
                cells,
                lax.ppermute(head, axis, [((i + 1) % count, i) for i in range(ends)]),
            ],
            axis=dim,
        )
    return cells


def pick_kernels(kernel_ids, kernels):
    table_size = kernels.shape[0]
    tile_edge = kernels.shape[1]
    onehot = (kernel_ids[..., None] == jnp.arange(table_size, dtype=jnp.int32)).astype(jnp.bfloat16)
    onehot = onehot.reshape(-1, table_size)
    selected = jnp.dot(onehot, kernels.reshape(table_size, -1), preferred_element_type=jnp.float32)
    selected = selected.astype(jnp.bfloat16).reshape(kernel_ids.shape + (tile_edge, tile_edge))
    return (selected[..., 0, :, :], selected[..., 1, :, :])


def adjoint_tiles(fetched, left_kernels, right_kernels, tile_weights, observed):
    left_product = jnp.einsum(
        "fetu,fuv->fetv", left_kernels, fetched, preferred_element_type=jnp.float32
    ).astype(jnp.bfloat16)
    predicted = jnp.einsum(
        "fetv,fewv->fetw", left_product, right_kernels, preferred_element_type=jnp.float32
    )
    residual = tile_weights.astype(jnp.float32)[..., None, None] * (
        predicted - observed.astype(jnp.float32)
    )
    residual = residual.astype(jnp.bfloat16)
    back_product = jnp.einsum(
        "feut,feuw->fetw", left_kernels, residual, preferred_element_type=jnp.float32
    ).astype(jnp.bfloat16)
    summed = jnp.sum(
        jnp.einsum(
            "fetw,fewv->fetv", back_product, right_kernels, preferred_element_type=jnp.float32
        ),
        axis=1,
    )
    return summed.astype(jnp.bfloat16)


def laplace_image(padded):
    image_rows = padded.reshape(padded.shape[0] * padded.shape[1], padded.shape[2])
    center = image_rows[:, 1:-1]
    vertical = jnp.pad(center, ((1, 1), (0, 0)))
    laplacian = 4.0 * center - image_rows[:, :-2] - image_rows[:, 2:] - vertical[:-2] - vertical[2:]
    return laplacian.reshape(padded.shape[0], padded.shape[1], padded.shape[2] - 2)


def per_device(
    sky_start, exposures, weights, footprint_owner, footprint_row, kernel_index, kernels
):
    sky_rows = sky_start.shape[0]
    tile_edge = sky_start.shape[1]
    foot_tiles = footprint_row.shape[1]
    expo_count = exposures.shape[2]
    n_sky = lax.axis_size("sky")
    n_exp = lax.axis_size("exp")
    capacity = max(2, 3 * foot_tiles // (2 * n_sky))
    slot_count = n_sky * capacity
    prior_weight = n_exp * foot_tiles * expo_count / (8.0 * sky_rows)
    owner_ids = footprint_owner[0, :, 0]
    tile_rows = footprint_row[0]
    onehot_owner = (owner_ids[:, None] == jnp.arange(n_sky, dtype=jnp.int32)[None, :]).astype(
        jnp.int32
    )
    ranks = jnp.sum((jnp.cumsum(onehot_owner, axis=0) - onehot_owner) * onehot_owner, axis=1)
    slot_of = owner_ids * capacity + ranks
    packing = jnp.arange(slot_count, dtype=jnp.int32)[:, None] == slot_of[None, :]
    requested = jnp.sum(jnp.where(packing, tile_rows[None, :] + 1, 0), axis=1) - 1
    slot_source = jnp.sum(jnp.where(packing, jnp.arange(foot_tiles)[None, :] + 1, 0), axis=1) - 1
    slot_source = jnp.where(slot_source < 0, foot_tiles, slot_source)
    observed = exposures[0]
    tile_weights = weights[0]
    kernel_ids = kernel_index[0]
    incoming = lax.all_to_all(requested, "sky", split_axis=0, concat_axis=0, tiled=True)
    left_kernels, right_kernels = pick_kernels(kernel_ids, kernels)
    receive_map = jnp.arange(sky_rows, dtype=jnp.int32)[:, None] == incoming[None, :]
    local_counts = float(expo_count) * jnp.sum(receive_map.astype(jnp.float32), axis=1)
    receive_half = receive_map.astype(jnp.bfloat16)
    safe_rows = jnp.maximum(incoming, 0)
    rows_per = sky_rows // n_exp
    own_rows = lax.axis_index("exp") * rows_per
    count_block = jnp.broadcast_to(
        local_counts.astype(jnp.bfloat16)[None, :, None], (n_exp, sky_rows, tile_edge)
    )
    half_edge = tile_edge // 2

    def exchange(outgoing_rows, extra, arrived_already=False):
        arrived = outgoing_rows
        if not arrived_already:
            arrived = lax.all_to_all(outgoing_rows, "sky", split_axis=0, concat_axis=0, tiled=True)
        partial_value = jnp.einsum(
            "rj,juv->ruv", receive_half, arrived, preferred_element_type=jnp.float32
        )
        payload = partial_value.astype(jnp.bfloat16).reshape(
            n_exp, rows_per * outgoing_rows.shape[1], tile_edge
        )
        if extra is not None:
            payload = jnp.concatenate([payload, extra], axis=1)
        row_parts = lax.all_to_all(payload, "exp", split_axis=0, concat_axis=0, tiled=True)
        return jnp.sum(row_parts.astype(jnp.float32).reshape((n_exp,) + payload.shape[1:]), axis=0)

    def fetch(part):
        replies = lax.all_to_all(
            part.astype(jnp.bfloat16)[safe_rows], "sky", split_axis=0, concat_axis=0, tiled=True
        )
        return replies[slot_of]

    def gather_scaled(summed, own_denominator):
        piece_edge = summed.shape[0] // rows_per
        own_total = summed.reshape(rows_per, piece_edge, tile_edge)
        scaled = (own_total / own_denominator[:, None, None]).astype(jnp.bfloat16)
        return scaled

    sky_now = sky_start
    fetched = None
    for iteration in range(ITERS):
        if fetched is None:
            fetched = fetch(sky_now)
        adjoint = adjoint_tiles(fetched, left_kernels, right_kernels, tile_weights, observed)
        padded_adjoint = jnp.concatenate(
            [adjoint, jnp.zeros((1, tile_edge, tile_edge), adjoint.dtype)], axis=0
        )
        outgoing = padded_adjoint[slot_source]
        laplacian = laplace_image(padded_2(sky_now, (("sky", 2),), 1))
        if iteration == 0:
            summed = exchange(outgoing[:, :half_edge], count_block)
            counts = summed[rows_per * half_edge :, 0]
            denominator = weight_ceiling * counts + 8.0 * prior_weight
            own_denominator = lax.dynamic_slice_in_dim(denominator, own_rows, rows_per)
            summed_head = summed[: rows_per * half_edge]
            smooth = prior_weight * laplacian / denominator[:, None, None]
        else:
            smooth = prior_weight * laplacian / denominator[:, None, None]
            if iteration + 1 == ITERS:
                scaled = gather_scaled(exchange(outgoing, None), own_denominator)
                gathered = lax.all_gather(scaled, "exp", axis=0, tiled=True)
                sky_now = sky_now - (gathered.astype(jnp.float32) + smooth)
                continue
            summed_head = exchange(outgoing[:, :half_edge], None)
        scaled_head = gather_scaled(summed_head, own_denominator)
        scaled_head, outgoing_tail = lax.optimization_barrier(
            (scaled_head, outgoing[:, half_edge:])
        )
        gathered_head = lax.all_gather(scaled_head, "exp", axis=0, tiled=True)
        arrived_tail = lax.all_to_all(outgoing_tail, "sky", split_axis=0, concat_axis=0, tiled=True)
        gathered_head, arrived_tail = lax.optimization_barrier((gathered_head, arrived_tail))
        scaled_tail = gather_scaled(exchange(arrived_tail, None, True), own_denominator)
        sky_head = sky_now[:, :half_edge] - (
            gathered_head.astype(jnp.float32) + smooth[:, :half_edge]
        )
        if iteration + 1 == ITERS:
            gathered_tail = lax.all_gather(scaled_tail, "exp", axis=0, tiled=True)
            sky_tail = sky_now[:, half_edge:] - (
                gathered_tail.astype(jnp.float32) + smooth[:, half_edge:]
            )
            sky_now = jnp.concatenate([sky_head, sky_tail], axis=1)
            continue
        request_head = sky_head.astype(jnp.bfloat16)[safe_rows]
        request_head, scaled_tail = lax.optimization_barrier((request_head, scaled_tail))
        gathered_tail = lax.all_gather(scaled_tail, "exp", axis=0, tiled=True)
        fetched_head = lax.all_to_all(
            request_head, "sky", split_axis=0, concat_axis=0, tiled=True
        )[slot_of]
        gathered_tail, fetched_head = lax.optimization_barrier((gathered_tail, fetched_head))
        sky_tail = sky_now[:, half_edge:] - (
            gathered_tail.astype(jnp.float32) + smooth[:, half_edge:]
        )
        fetched = jnp.concatenate([fetched_head, fetch(sky_tail)], axis=1)
        sky_now = jnp.concatenate([sky_head, sky_tail], axis=1)
    return sky_now


def solution(mesh):
    in_specs = (
        P(None, None, "sky"),
        P("exp", "sky", None, None, None),
        P("exp", "sky", None),
        P("exp", "sky", None),
        P("exp", "sky"),
        P("exp", "sky", None, None),
        P(),
    )
    out_specs = P(None, None, "sky")
    return jax.shard_map(
        per_device, mesh=mesh, in_specs=in_specs, out_specs=out_specs, check_vma=False
    )
```

```python
import jax
import jax.numpy as jnp
from jax import lax
from jax.sharding import PartitionSpec as P
from jax.experimental import pallas as pl
from jax.experimental.pallas import tpu as pltpu

ITERS = 2


weight_ceiling = 2.0


def padded_2(cells, sides, width):
    for axis, dim in sides:
        count = lax.axis_size(axis)
        ends = count - 1
        head = lax.slice_in_dim(cells, 0, width, axis=dim)
        tail = lax.slice_in_dim(cells, cells.shape[dim] - width, cells.shape[dim], axis=dim)
        cells = jnp.concatenate(
            [
                lax.ppermute(tail, axis, [(i, (i + 1) % count) for i in range(ends)]),
                cells,
                lax.ppermute(head, axis, [((i + 1) % count, i) for i in range(ends)]),
            ],
            axis=dim,
        )
    return cells


def pick_kernels(kernel_ids, kernels):
    table_size = kernels.shape[0]
    tile_edge = kernels.shape[1]
    onehot = (kernel_ids[..., None] == jnp.arange(table_size, dtype=jnp.int32)).astype(jnp.bfloat16)
    onehot = onehot.reshape(-1, table_size)
    selected = jnp.dot(onehot, kernels.reshape(table_size, -1), preferred_element_type=jnp.float32)
    selected = selected.astype(jnp.bfloat16).reshape(kernel_ids.shape + (tile_edge, tile_edge))
    return (selected[..., 0, :, :], selected[..., 1, :, :])


def adjoint_tiles(fetched, left_kernels, right_kernels, tile_weights, observed):
    left_product = jnp.einsum(
        "fetu,fuv->fetv", left_kernels, fetched, preferred_element_type=jnp.float32
    ).astype(jnp.bfloat16)
    predicted = jnp.einsum(
        "fetv,fewv->fetw", left_product, right_kernels, preferred_element_type=jnp.float32
    )
    residual = tile_weights.astype(jnp.float32)[..., None, None] * (
        predicted - observed.astype(jnp.float32)
    )
    residual = residual.astype(jnp.bfloat16)
    back_product = jnp.einsum(
        "feut,feuw->fetw", left_kernels, residual, preferred_element_type=jnp.float32
    ).astype(jnp.bfloat16)
    summed = jnp.sum(
        jnp.einsum(
            "fetw,fewv->fetv", back_product, right_kernels, preferred_element_type=jnp.float32
        ),
        axis=1,
    )
    return summed.astype(jnp.bfloat16)


def chain_kernel(ids_ref, weight_ref, fetched_ref, observed_ref, table_ref, flipped_ref, out_ref):
    block = fetched_ref.shape[0]
    expo_count = observed_ref.shape[1]
    base = pl.program_id(0) * block
    for j in range(block):
        sky_tile = fetched_ref[j]
        total = None
        for e in range(expo_count):
            slot = (base + j) * expo_count + e
            left_id = ids_ref[2 * slot]
            right_id = ids_ref[2 * slot + 1]
            left_product = jnp.dot(
                table_ref[left_id], sky_tile, preferred_element_type=jnp.float32
            ).astype(jnp.bfloat16)
            predicted = jnp.dot(
                left_product, flipped_ref[right_id], preferred_element_type=jnp.float32
            )
            residual = weight_ref[slot] * (predicted - observed_ref[j, e].astype(jnp.float32))
            back_product = jnp.dot(
                flipped_ref[left_id],
                residual.astype(jnp.bfloat16),
                preferred_element_type=jnp.float32,
            ).astype(jnp.bfloat16)
            term = jnp.dot(back_product, table_ref[right_id], preferred_element_type=jnp.float32)
            total = term if total is None else total + term
        out_ref[j] = total.astype(jnp.bfloat16)


def adjoint_chain(fetched, kernel_ids, kernels, tile_weights, observed):
    foot_tiles, tile_edge = fetched.shape[0], fetched.shape[1]
    expo_count = observed.shape[1]
    table_size = kernels.shape[0]
    block = 8 if foot_tiles % 8 == 0 else 1
    flipped = jnp.swapaxes(kernels, 1, 2)
    return pl.pallas_call(
        chain_kernel,
        grid_spec=pltpu.PrefetchScalarGridSpec(
            num_scalar_prefetch=1,
            grid=(foot_tiles // block,),
            in_specs=[
                pl.BlockSpec(memory_space=pltpu.SMEM),
                pl.BlockSpec((block, tile_edge, tile_edge), lambda i, ids: (i, 0, 0)),
                pl.BlockSpec(
                    (block, expo_count, tile_edge, tile_edge), lambda i, ids: (i, 0, 0, 0)
                ),
                pl.BlockSpec((table_size, tile_edge, tile_edge), lambda i, ids: (0, 0, 0)),
                pl.BlockSpec((table_size, tile_edge, tile_edge), lambda i, ids: (0, 0, 0)),
            ],
            out_specs=pl.BlockSpec((block, tile_edge, tile_edge), lambda i, ids: (i, 0, 0)),
        ),
        out_shape=jax.ShapeDtypeStruct((foot_tiles, tile_edge, tile_edge), jnp.bfloat16),
    )(
        kernel_ids.reshape(-1),
        tile_weights.astype(jnp.float32).reshape(-1),
        fetched,
        observed,
        kernels,
        flipped,
    )


def laplace_image(padded):
    image_rows = padded.reshape(padded.shape[0] * padded.shape[1], padded.shape[2])
    center = image_rows[:, 1:-1]
    vertical = jnp.pad(center, ((1, 1), (0, 0)))
    laplacian = 4.0 * center - image_rows[:, :-2] - image_rows[:, 2:] - vertical[:-2] - vertical[2:]
    return laplacian.reshape(padded.shape[0], padded.shape[1], padded.shape[2] - 2)


def per_device(
    sky_start, exposures, weights, footprint_owner, footprint_row, kernel_index, kernels
):
    sky_rows = sky_start.shape[0]
    tile_edge = sky_start.shape[1]
    foot_tiles = footprint_row.shape[1]
    expo_count = exposures.shape[2]
    n_sky = lax.axis_size("sky")
    n_exp = lax.axis_size("exp")
    capacity = max(2, 3 * foot_tiles // (2 * n_sky))
    slot_count = n_sky * capacity
    prior_weight = n_exp * foot_tiles * expo_count / (8.0 * sky_rows)
    owner_ids = footprint_owner[0, :, 0]
    tile_rows = footprint_row[0]
    onehot_owner = (owner_ids[:, None] == jnp.arange(n_sky, dtype=jnp.int32)[None, :]).astype(
        jnp.int32
    )
    ranks = jnp.sum((jnp.cumsum(onehot_owner, axis=0) - onehot_owner) * onehot_owner, axis=1)
    slot_of = owner_ids * capacity + ranks
    packing = jnp.arange(slot_count, dtype=jnp.int32)[:, None] == slot_of[None, :]
    requested = jnp.sum(jnp.where(packing, tile_rows[None, :] + 1, 0), axis=1) - 1
    slot_source = jnp.sum(jnp.where(packing, jnp.arange(foot_tiles)[None, :] + 1, 0), axis=1) - 1
    slot_source = jnp.where(slot_source < 0, foot_tiles, slot_source)
    observed = exposures[0]
    tile_weights = weights[0]
    kernel_ids = kernel_index[0]
    incoming = lax.all_to_all(requested, "sky", split_axis=0, concat_axis=0, tiled=True)
    receive_map = jnp.arange(sky_rows, dtype=jnp.int32)[:, None] == incoming[None, :]
    local_counts = float(expo_count) * jnp.sum(receive_map.astype(jnp.float32), axis=1)
    receive_half = receive_map.astype(jnp.bfloat16)
    safe_rows = jnp.maximum(incoming, 0)
    rows_per = sky_rows // n_exp
    own_rows = lax.axis_index("exp") * rows_per
    count_block = jnp.broadcast_to(
        local_counts.astype(jnp.bfloat16)[None, :, None], (n_exp, sky_rows, tile_edge)
    )
    sky_now = sky_start
    for iteration in range(ITERS):
        sky_half = sky_now.astype(jnp.bfloat16)
        replies = lax.all_to_all(
            sky_half[safe_rows], "sky", split_axis=0, concat_axis=0, tiled=True
        )
        fetched = replies[slot_of]
        adjoint = adjoint_chain(fetched, kernel_ids, kernels, tile_weights, observed)
        padded_adjoint = jnp.concatenate(
            [adjoint, jnp.zeros((1, tile_edge, tile_edge), adjoint.dtype)], axis=0
        )
        outgoing = padded_adjoint[slot_source]
        arrived = lax.all_to_all(outgoing, "sky", split_axis=0, concat_axis=0, tiled=True)
        partial_value = jnp.einsum(
            "rj,juv->ruv", receive_half, arrived, preferred_element_type=jnp.float32
        )
        payload = partial_value.astype(jnp.bfloat16).reshape(n_exp, rows_per * tile_edge, tile_edge)
        if iteration == 0:
            payload = jnp.concatenate([payload, count_block], axis=1)
        row_parts = lax.all_to_all(payload, "exp", split_axis=0, concat_axis=0, tiled=True)
        summed = jnp.sum(row_parts.astype(jnp.float32).reshape((n_exp,) + payload.shape[1:]), axis=0)
        if iteration == 0:
            counts = summed[rows_per * tile_edge :, 0]
            denominator = weight_ceiling * counts + 8.0 * prior_weight
            own_denominator = lax.dynamic_slice_in_dim(denominator, own_rows, rows_per)
        own_total = summed[: rows_per * tile_edge].reshape(rows_per, tile_edge, tile_edge)
        scaled = own_total / own_denominator[:, None, None]
        gathered = lax.all_gather(scaled.astype(jnp.bfloat16), "exp", axis=0, tiled=True)
        laplacian = laplace_image(padded_2(sky_now, (("sky", 2),), 1))
        smooth = prior_weight * laplacian / denominator[:, None, None]
        sky_now = sky_now - (gathered.astype(jnp.float32) + smooth)
    return sky_now


def solution(mesh):
    in_specs = (
        P(None, None, "sky"),
        P("exp", "sky", None, None, None),
        P("exp", "sky", None),
        P("exp", "sky", None),
        P("exp", "sky"),
        P("exp", "sky", None, None),
        P(),
    )
    out_specs = P(None, None, "sky")
    return jax.shard_map(
        per_device, mesh=mesh, in_specs=in_specs, out_specs=out_specs, check_vma=False
    )
```

```python
import jax
import jax.numpy as jnp
from jax import lax
from jax.sharding import PartitionSpec as P

ITERS = 2


weight_ceiling = 2.0


def padded_2(cells, sides, width):
    for axis, dim in sides:
        count = lax.axis_size(axis)
        ends = count - 1
        head = lax.slice_in_dim(cells, 0, width, axis=dim)
        tail = lax.slice_in_dim(cells, cells.shape[dim] - width, cells.shape[dim], axis=dim)
        cells = jnp.concatenate(
            [
                lax.ppermute(tail, axis, [(i, (i + 1) % count) for i in range(ends)]),
                cells,
                lax.ppermute(head, axis, [((i + 1) % count, i) for i in range(ends)]),
            ],
            axis=dim,
        )
    return cells


def pick_kernels(kernel_ids, kernels):
    table_size = kernels.shape[0]
    tile_edge = kernels.shape[1]
    onehot = (kernel_ids[..., None] == jnp.arange(table_size, dtype=jnp.int32)).astype(jnp.bfloat16)
    onehot = onehot.reshape(-1, table_size)
    selected = jnp.dot(onehot, kernels.reshape(table_size, -1), preferred_element_type=jnp.float32)
    selected = selected.astype(jnp.bfloat16).reshape(kernel_ids.shape + (tile_edge, tile_edge))
    return (selected[..., 0, :, :], selected[..., 1, :, :])


def adjoint_tiles(fetched, left_kernels, right_kernels, tile_weights, observed):
    left_product = jnp.einsum(
        "fetu,fuv->fetv", left_kernels, fetched, preferred_element_type=jnp.float32
    ).astype(jnp.bfloat16)
    predicted = jnp.einsum(
        "fetv,fewv->fetw", left_product, right_kernels, preferred_element_type=jnp.float32
    )
    residual = tile_weights.astype(jnp.float32)[..., None, None] * (
        predicted - observed.astype(jnp.float32)
    )
    residual = residual.astype(jnp.bfloat16)
    back_product = jnp.einsum(
        "feut,feuw->fetw", left_kernels, residual, preferred_element_type=jnp.float32
    ).astype(jnp.bfloat16)
    summed = jnp.sum(
        jnp.einsum(
            "fetw,fewv->fetv", back_product, right_kernels, preferred_element_type=jnp.float32
        ),
        axis=1,
    )
    return summed.astype(jnp.bfloat16)


def laplace_image(padded):
    image_rows = padded.reshape(padded.shape[0] * padded.shape[1], padded.shape[2])
    center = image_rows[:, 1:-1]
    vertical = jnp.pad(center, ((1, 1), (0, 0)))
    laplacian = 4.0 * center - image_rows[:, :-2] - image_rows[:, 2:] - vertical[:-2] - vertical[2:]
    return laplacian.reshape(padded.shape[0], padded.shape[1], padded.shape[2] - 2)


def per_device(
    sky_start, exposures, weights, footprint_owner, footprint_row, kernel_index, kernels
):
    sky_rows = sky_start.shape[0]
    tile_edge = sky_start.shape[1]
    foot_tiles = footprint_row.shape[1]
    expo_count = exposures.shape[2]
    n_sky = lax.axis_size("sky")
    n_exp = lax.axis_size("exp")
    capacity = max(2, 3 * foot_tiles // (2 * n_sky))
    slot_count = n_sky * capacity
    prior_weight = n_exp * foot_tiles * expo_count / (8.0 * sky_rows)
    owner_ids = footprint_owner[0, :, 0]
    tile_rows = footprint_row[0]
    onehot_owner = (owner_ids[:, None] == jnp.arange(n_sky, dtype=jnp.int32)[None, :]).astype(
        jnp.int32
    )
    ranks = jnp.sum((jnp.cumsum(onehot_owner, axis=0) - onehot_owner) * onehot_owner, axis=1)
    slot_of = owner_ids * capacity + ranks
    packing = jnp.arange(slot_count, dtype=jnp.int32)[:, None] == slot_of[None, :]
    requested = jnp.sum(jnp.where(packing, tile_rows[None, :] + 1, 0), axis=1) - 1
    slot_source = jnp.sum(jnp.where(packing, jnp.arange(foot_tiles)[None, :] + 1, 0), axis=1) - 1
    slot_source = jnp.where(slot_source < 0, foot_tiles, slot_source)
    observed = exposures[0]
    tile_weights = weights[0]
    kernel_ids = kernel_index[0]
    incoming = lax.all_to_all(requested, "sky", split_axis=0, concat_axis=0, tiled=True)
    left_kernels, right_kernels = pick_kernels(kernel_ids, kernels)
    receive_map = jnp.arange(sky_rows, dtype=jnp.int32)[:, None] == incoming[None, :]
    local_counts = float(expo_count) * jnp.sum(receive_map.astype(jnp.float32), axis=1)
    receive_half = receive_map.astype(jnp.bfloat16)
    safe_rows = jnp.maximum(incoming, 0)
    rows_per = sky_rows // n_exp
    own_rows = lax.axis_index("exp") * rows_per
    count_tile = jnp.broadcast_to(
        local_counts[:, None], (sky_rows, tile_edge)
    )
    sky_now = sky_start
    for iteration in range(ITERS):
        sky_half = sky_now.astype(jnp.bfloat16)
        replies = lax.all_to_all(
            sky_half[safe_rows], "sky", split_axis=0, concat_axis=0, tiled=True
        )
        if iteration == 0:
            count_tiles = lax.all_gather(count_tile, "exp", axis=0, tiled=True)
            count_tiles, replies = lax.optimization_barrier((count_tiles, replies))
            counts = jnp.sum(
                count_tiles.astype(jnp.float32).reshape(n_exp, sky_rows, tile_edge)[:, :, 0], axis=0
            )
            denominator = weight_ceiling * counts + 8.0 * prior_weight
            own_denominator = lax.dynamic_slice_in_dim(denominator, own_rows, rows_per)
        fetched = replies[slot_of]
        adjoint = adjoint_tiles(fetched, left_kernels, right_kernels, tile_weights, observed)
        padded_adjoint = jnp.concatenate(
            [adjoint, jnp.zeros((1, tile_edge, tile_edge), adjoint.dtype)], axis=0
        )
        outgoing = padded_adjoint[slot_source]
        arrived = lax.all_to_all(outgoing, "sky", split_axis=0, concat_axis=0, tiled=True)
        partial_value = jnp.einsum(
            "rj,juv->ruv", receive_half, arrived, preferred_element_type=jnp.float32
        )
        payload = partial_value.astype(jnp.bfloat16).reshape(n_exp, rows_per * tile_edge, tile_edge)
        row_parts = lax.all_to_all(payload, "exp", split_axis=0, concat_axis=0, tiled=True)
        summed = jnp.sum(row_parts.astype(jnp.float32).reshape((n_exp,) + payload.shape[1:]), axis=0)
        own_total = summed[: rows_per * tile_edge].reshape(rows_per, tile_edge, tile_edge)
        scaled = own_total / own_denominator[:, None, None]
        gathered = lax.all_gather(scaled.astype(jnp.bfloat16), "exp", axis=0, tiled=True)
        laplacian = laplace_image(padded_2(sky_now, (("sky", 2),), 1))
        smooth = prior_weight * laplacian / denominator[:, None, None]
        sky_now = sky_now - (gathered.astype(jnp.float32) + smooth)
    return sky_now


def solution(mesh):
    in_specs = (
        P(None, None, "sky"),
        P("exp", "sky", None, None, None),
        P("exp", "sky", None),
        P("exp", "sky", None),
        P("exp", "sky"),
        P("exp", "sky", None, None),
        P(),
    )
    out_specs = P(None, None, "sky")
    return jax.shard_map(
        per_device, mesh=mesh, in_specs=in_specs, out_specs=out_specs, check_vma=False
    )
```

```python
import jax
import jax.numpy as jnp
from jax import lax
from jax.sharding import PartitionSpec as P

ITERS = 2


weight_ceiling = 2.0


def padded_2(cells, sides, width):
    for axis, dim in sides:
        count = lax.axis_size(axis)
        ends = count - 1
        head = lax.slice_in_dim(cells, 0, width, axis=dim)
        tail = lax.slice_in_dim(cells, cells.shape[dim] - width, cells.shape[dim], axis=dim)
        cells = jnp.concatenate(
            [
                lax.ppermute(tail, axis, [(i, (i + 1) % count) for i in range(ends)]),
                cells,
                lax.ppermute(head, axis, [((i + 1) % count, i) for i in range(ends)]),
            ],
            axis=dim,
        )
    return cells


def pick_kernels(kernel_ids, kernels):
    table_size = kernels.shape[0]
    tile_edge = kernels.shape[1]
    onehot = (kernel_ids[..., None] == jnp.arange(table_size, dtype=jnp.int32)).astype(jnp.bfloat16)
    onehot = onehot.reshape(-1, table_size)
    selected = jnp.dot(onehot, kernels.reshape(table_size, -1), preferred_element_type=jnp.float32)
    selected = selected.astype(jnp.bfloat16).reshape(kernel_ids.shape + (tile_edge, tile_edge))
    return (selected[..., 0, :, :], selected[..., 1, :, :])


def adjoint_tiles(fetched, left_kernels, right_kernels, tile_weights, observed):
    left_product = jnp.einsum(
        "fetu,fuv->fetv", left_kernels, fetched, preferred_element_type=jnp.float32
    ).astype(jnp.bfloat16)
    predicted = jnp.einsum(
        "fetv,fewv->fetw", left_product, right_kernels, preferred_element_type=jnp.float32
    )
    residual = tile_weights.astype(jnp.float32)[..., None, None] * (
        predicted - observed.astype(jnp.float32)
    )
    residual = residual.astype(jnp.bfloat16)
    back_product = jnp.einsum(
        "feut,feuw->fetw", left_kernels, residual, preferred_element_type=jnp.float32
    ).astype(jnp.bfloat16)
    summed = jnp.sum(
        jnp.einsum(
            "fetw,fewv->fetv", back_product, right_kernels, preferred_element_type=jnp.float32
        ),
        axis=1,
    )
    return summed.astype(jnp.bfloat16)


def laplace_image(padded):
    image_rows = padded.reshape(padded.shape[0] * padded.shape[1], padded.shape[2])
    center = image_rows[:, 1:-1]
    vertical = jnp.pad(center, ((1, 1), (0, 0)))
    laplacian = 4.0 * center - image_rows[:, :-2] - image_rows[:, 2:] - vertical[:-2] - vertical[2:]
    return laplacian.reshape(padded.shape[0], padded.shape[1], padded.shape[2] - 2)


def per_device(
    sky_start, exposures, weights, footprint_owner, footprint_row, kernel_index, kernels
):
    sky_rows = sky_start.shape[0]
    tile_edge = sky_start.shape[1]
    foot_tiles = footprint_row.shape[1]
    expo_count = exposures.shape[2]
    n_sky = lax.axis_size("sky")
    n_exp = lax.axis_size("exp")
    capacity = max(2, 3 * foot_tiles // (2 * n_sky))
    slot_count = n_sky * capacity
    prior_weight = n_exp * foot_tiles * expo_count / (8.0 * sky_rows)
    owner_ids = footprint_owner[0, :, 0]
    tile_rows = footprint_row[0]
    onehot_owner = (owner_ids[:, None] == jnp.arange(n_sky, dtype=jnp.int32)[None, :]).astype(
        jnp.int32
    )
    ranks = jnp.sum((jnp.cumsum(onehot_owner, axis=0) - onehot_owner) * onehot_owner, axis=1)
    slot_of = owner_ids * capacity + ranks
    packing = jnp.arange(slot_count, dtype=jnp.int32)[:, None] == slot_of[None, :]
    requested = jnp.sum(jnp.where(packing, tile_rows[None, :] + 1, 0), axis=1) - 1
    slot_source = jnp.sum(jnp.where(packing, jnp.arange(foot_tiles)[None, :] + 1, 0), axis=1) - 1
    slot_source = jnp.where(slot_source < 0, foot_tiles, slot_source)
    observed = exposures[0]
    tile_weights = weights[0]
    kernel_ids = kernel_index[0]
    incoming = lax.all_to_all(requested, "sky", split_axis=0, concat_axis=0, tiled=True)
    left_kernels, right_kernels = pick_kernels(kernel_ids, kernels)
    receive_map = jnp.arange(sky_rows, dtype=jnp.int32)[:, None] == incoming[None, :]
    local_counts = float(expo_count) * jnp.sum(receive_map.astype(jnp.float32), axis=1)
    receive_half = receive_map.astype(jnp.bfloat16)
    safe_rows = jnp.maximum(incoming, 0)
    rows_per = sky_rows // n_exp
    own_rows = lax.axis_index("exp") * rows_per
    count_tile = jnp.broadcast_to(
        local_counts[:, None], (sky_rows, tile_edge)
    )
    sky_now = sky_start
    for iteration in range(ITERS):
        sky_half = sky_now.astype(jnp.bfloat16)
        replies = lax.all_to_all(
            sky_half[safe_rows], "sky", split_axis=0, concat_axis=0, tiled=True
        )
        fetched = replies[slot_of]
        adjoint = adjoint_tiles(fetched, left_kernels, right_kernels, tile_weights, observed)
        padded_adjoint = jnp.concatenate(
            [adjoint, jnp.zeros((1, tile_edge, tile_edge), adjoint.dtype)], axis=0
        )
        outgoing = padded_adjoint[slot_source]
        arrived = lax.all_to_all(outgoing, "sky", split_axis=0, concat_axis=0, tiled=True)
        if iteration == 0:
            count_tiles = lax.all_gather(count_tile, "exp", axis=0, tiled=True)
            count_tiles, arrived = lax.optimization_barrier((count_tiles, arrived))
            counts = jnp.sum(
                count_tiles.astype(jnp.float32).reshape(n_exp, sky_rows, tile_edge)[:, :, 0], axis=0
            )
            denominator = weight_ceiling * counts + 8.0 * prior_weight
            own_denominator = lax.dynamic_slice_in_dim(denominator, own_rows, rows_per)
        partial_value = jnp.einsum(
            "rj,juv->ruv", receive_half, arrived, preferred_element_type=jnp.float32
        )
        payload = partial_value.astype(jnp.bfloat16).reshape(n_exp, rows_per * tile_edge, tile_edge)
        row_parts = lax.all_to_all(payload, "exp", split_axis=0, concat_axis=0, tiled=True)
        summed = jnp.sum(row_parts.astype(jnp.float32).reshape((n_exp,) + payload.shape[1:]), axis=0)
        own_total = summed[: rows_per * tile_edge].reshape(rows_per, tile_edge, tile_edge)
        scaled = own_total / own_denominator[:, None, None]
        gathered = lax.all_gather(scaled.astype(jnp.bfloat16), "exp", axis=0, tiled=True)
        laplacian = laplace_image(padded_2(sky_now, (("sky", 2),), 1))
        smooth = prior_weight * laplacian / denominator[:, None, None]
        sky_now = sky_now - (gathered.astype(jnp.float32) + smooth)
    return sky_now


def solution(mesh):
    in_specs = (
        P(None, None, "sky"),
        P("exp", "sky", None, None, None),
        P("exp", "sky", None),
        P("exp", "sky", None),
        P("exp", "sky"),
        P("exp", "sky", None, None),
        P(),
    )
    out_specs = P(None, None, "sky")
    return jax.shard_map(
        per_device, mesh=mesh, in_specs=in_specs, out_specs=out_specs, check_vma=False
    )
```

```python
import jax
import jax.numpy as jnp
from jax import lax
from jax.sharding import PartitionSpec as P

ITERS = 2


weight_ceiling = 2.0


def padded_2(cells, sides, width):
    for axis, dim in sides:
        count = lax.axis_size(axis)
        ends = count - 1
        head = lax.slice_in_dim(cells, 0, width, axis=dim)
        tail = lax.slice_in_dim(cells, cells.shape[dim] - width, cells.shape[dim], axis=dim)
        cells = jnp.concatenate(
            [
                lax.ppermute(tail, axis, [(i, (i + 1) % count) for i in range(ends)]),
                cells,
                lax.ppermute(head, axis, [((i + 1) % count, i) for i in range(ends)]),
            ],
            axis=dim,
        )
    return cells


def pick_kernels(kernel_ids, kernels):
    table_size = kernels.shape[0]
    tile_edge = kernels.shape[1]
    onehot = (kernel_ids[..., None] == jnp.arange(table_size, dtype=jnp.int32)).astype(jnp.bfloat16)
    onehot = onehot.reshape(-1, table_size)
    selected = jnp.dot(onehot, kernels.reshape(table_size, -1), preferred_element_type=jnp.float32)
    selected = selected.astype(jnp.bfloat16).reshape(kernel_ids.shape + (tile_edge, tile_edge))
    return (selected[..., 0, :, :], selected[..., 1, :, :])


def adjoint_tiles(fetched, left_kernels, right_kernels, tile_weights, observed):
    left_product = jnp.einsum(
        "fetu,fuv->fetv", left_kernels, fetched, preferred_element_type=jnp.float32
    ).astype(jnp.bfloat16)
    predicted = jnp.einsum(
        "fetv,fewv->fetw", left_product, right_kernels, preferred_element_type=jnp.float32
    )
    residual = tile_weights.astype(jnp.float32)[..., None, None] * (
        predicted - observed.astype(jnp.float32)
    )
    residual = residual.astype(jnp.bfloat16)
    back_product = jnp.einsum(
        "feut,feuw->fetw", left_kernels, residual, preferred_element_type=jnp.float32
    ).astype(jnp.bfloat16)
    summed = jnp.sum(
        jnp.einsum(
            "fetw,fewv->fetv", back_product, right_kernels, preferred_element_type=jnp.float32
        ),
        axis=1,
    )
    return summed.astype(jnp.bfloat16)


def laplace_image(padded):
    image_rows = padded.reshape(padded.shape[0] * padded.shape[1], padded.shape[2])
    center = image_rows[:, 1:-1]
    vertical = jnp.pad(center, ((1, 1), (0, 0)))
    laplacian = 4.0 * center - image_rows[:, :-2] - image_rows[:, 2:] - vertical[:-2] - vertical[2:]
    return laplacian.reshape(padded.shape[0], padded.shape[1], padded.shape[2] - 2)


def per_device(
    sky_start, exposures, weights, footprint_owner, footprint_row, kernel_index, kernels
):
    sky_rows = sky_start.shape[0]
    tile_edge = sky_start.shape[1]
    foot_tiles = footprint_row.shape[1]
    expo_count = exposures.shape[2]
    n_sky = lax.axis_size("sky")
    n_exp = lax.axis_size("exp")
    capacity = max(2, 3 * foot_tiles // (2 * n_sky))
    slot_count = n_sky * capacity
    prior_weight = n_exp * foot_tiles * expo_count / (8.0 * sky_rows)
    owner_ids = footprint_owner[0, :, 0]
    tile_rows = footprint_row[0]
    onehot_owner = (owner_ids[:, None] == jnp.arange(n_sky, dtype=jnp.int32)[None, :]).astype(
        jnp.int32
    )
    ranks = jnp.sum((jnp.cumsum(onehot_owner, axis=0) - onehot_owner) * onehot_owner, axis=1)
    slot_of = owner_ids * capacity + ranks
    packing = jnp.arange(slot_count, dtype=jnp.int32)[:, None] == slot_of[None, :]
    requested = jnp.sum(jnp.where(packing, tile_rows[None, :] + 1, 0), axis=1) - 1
    slot_source = jnp.sum(jnp.where(packing, jnp.arange(foot_tiles)[None, :] + 1, 0), axis=1) - 1
    slot_source = jnp.where(slot_source < 0, foot_tiles, slot_source)
    observed = exposures[0]
    tile_weights = weights[0]
    kernel_ids = kernel_index[0]
    incoming = lax.all_to_all(requested, "sky", split_axis=0, concat_axis=0, tiled=True)
    left_kernels, right_kernels = pick_kernels(kernel_ids, kernels)
    receive_map = jnp.arange(sky_rows, dtype=jnp.int32)[:, None] == incoming[None, :]
    local_counts = float(expo_count) * jnp.sum(receive_map.astype(jnp.float32), axis=1)
    receive_half = receive_map.astype(jnp.bfloat16)
    safe_rows = jnp.maximum(incoming, 0)
    rows_per = sky_rows // n_exp
    own_rows = lax.axis_index("exp") * rows_per
    count_tile = jnp.broadcast_to(
        local_counts[:, None], (sky_rows, tile_edge)
    )
    sky_now = sky_start
    request = sky_now.astype(jnp.bfloat16)[safe_rows]
    for iteration in range(ITERS):
        replies = lax.all_to_all(request, "sky", split_axis=0, concat_axis=0, tiled=True)
        fetched = replies[slot_of]
        adjoint = adjoint_tiles(fetched, left_kernels, right_kernels, tile_weights, observed)
        padded_adjoint = jnp.concatenate(
            [adjoint, jnp.zeros((1, tile_edge, tile_edge), adjoint.dtype)], axis=0
        )
        outgoing = padded_adjoint[slot_source]
        arrived = lax.all_to_all(outgoing, "sky", split_axis=0, concat_axis=0, tiled=True)
        if iteration == 0:
            count_tiles = lax.all_gather(count_tile, "exp", axis=0, tiled=True)
            count_tiles, arrived = lax.optimization_barrier((count_tiles, arrived))
            counts = jnp.sum(
                count_tiles.astype(jnp.float32).reshape(n_exp, sky_rows, tile_edge)[:, :, 0], axis=0
            )
            denominator = weight_ceiling * counts + 8.0 * prior_weight
            own_denominator = lax.dynamic_slice_in_dim(denominator, own_rows, rows_per)
        partial_value = jnp.einsum(
            "rj,juv->ruv", receive_half, arrived, preferred_element_type=jnp.float32
        )
        payload = partial_value.astype(jnp.bfloat16).reshape(n_exp, rows_per * tile_edge, tile_edge)
        row_parts = lax.all_to_all(payload, "exp", split_axis=0, concat_axis=0, tiled=True)
        summed = jnp.sum(row_parts.astype(jnp.float32).reshape((n_exp,) + payload.shape[1:]), axis=0)
        own_total = summed[: rows_per * tile_edge].reshape(rows_per, tile_edge, tile_edge)
        scaled = own_total / own_denominator[:, None, None]
        gathered = lax.all_gather(scaled.astype(jnp.bfloat16), "exp", axis=0, tiled=True)
        laplacian = laplace_image(padded_2(sky_now, (("sky", 2),), 1))
        smooth = prior_weight * laplacian / denominator[:, None, None]
        if iteration + 1 < ITERS:
            request = (
                sky_now[safe_rows]
                - (gathered[safe_rows].astype(jnp.float32) + smooth[safe_rows])
            ).astype(jnp.bfloat16)
        sky_now = sky_now - (gathered.astype(jnp.float32) + smooth)
    return sky_now


def solution(mesh):
    in_specs = (
        P(None, None, "sky"),
        P("exp", "sky", None, None, None),
        P("exp", "sky", None),
        P("exp", "sky", None),
        P("exp", "sky"),
        P("exp", "sky", None, None),
        P(),
    )
    out_specs = P(None, None, "sky")
    return jax.shard_map(
        per_device, mesh=mesh, in_specs=in_specs, out_specs=out_specs, check_vma=False
    )
```

```python
import jax
import jax.numpy as jnp
from jax import lax
from jax.sharding import PartitionSpec as P

ITERS = 2


weight_ceiling = 2.0


def padded_2(cells, sides, width):
    for axis, dim in sides:
        count = lax.axis_size(axis)
        ends = count - 1
        head = lax.slice_in_dim(cells, 0, width, axis=dim)
        tail = lax.slice_in_dim(cells, cells.shape[dim] - width, cells.shape[dim], axis=dim)
        cells = jnp.concatenate(
            [
                lax.ppermute(tail, axis, [(i, (i + 1) % count) for i in range(ends)]),
                cells,
                lax.ppermute(head, axis, [((i + 1) % count, i) for i in range(ends)]),
            ],
            axis=dim,
        )
    return cells


def pick_kernels(kernel_ids, kernels):
    table_size = kernels.shape[0]
    tile_edge = kernels.shape[1]
    onehot = (kernel_ids[..., None] == jnp.arange(table_size, dtype=jnp.int32)).astype(jnp.bfloat16)
    onehot = onehot.reshape(-1, table_size)
    selected = jnp.dot(onehot, kernels.reshape(table_size, -1), preferred_element_type=jnp.float32)
    selected = selected.astype(jnp.bfloat16).reshape(kernel_ids.shape + (tile_edge, tile_edge))
    return (selected[..., 0, :, :], selected[..., 1, :, :])


def adjoint_tiles(fetched, left_kernels, right_kernels, tile_weights, observed):
    left_product = jnp.einsum(
        "fetu,fuv->fetv", left_kernels, fetched, preferred_element_type=jnp.float32
    ).astype(jnp.bfloat16)
    predicted = jnp.einsum(
        "fetv,fewv->fetw", left_product, right_kernels, preferred_element_type=jnp.float32
    )
    residual = tile_weights.astype(jnp.float32)[..., None, None] * (
        predicted - observed.astype(jnp.float32)
    )
    residual = residual.astype(jnp.bfloat16)
    back_product = jnp.einsum(
        "feut,feuw->fetw", left_kernels, residual, preferred_element_type=jnp.float32
    ).astype(jnp.bfloat16)
    summed = jnp.sum(
        jnp.einsum(
            "fetw,fewv->fetv", back_product, right_kernels, preferred_element_type=jnp.float32
        ),
        axis=1,
    )
    return summed.astype(jnp.bfloat16)


def laplace_image(padded):
    image_rows = padded.reshape(padded.shape[0] * padded.shape[1], padded.shape[2])
    center = image_rows[:, 1:-1]
    vertical = jnp.pad(center, ((1, 1), (0, 0)))
    laplacian = 4.0 * center - image_rows[:, :-2] - image_rows[:, 2:] - vertical[:-2] - vertical[2:]
    return laplacian.reshape(padded.shape[0], padded.shape[1], padded.shape[2] - 2)


def per_device(
    sky_start, exposures, weights, footprint_owner, footprint_row, kernel_index, kernels
):
    sky_rows = sky_start.shape[0]
    tile_edge = sky_start.shape[1]
    foot_tiles = footprint_row.shape[1]
    expo_count = exposures.shape[2]
    n_sky = lax.axis_size("sky")
    n_exp = lax.axis_size("exp_hi") * lax.axis_size("exp_lo")
    capacity = max(2, 3 * foot_tiles // (2 * n_sky))
    slot_count = n_sky * capacity
    prior_weight = n_exp * foot_tiles * expo_count / (8.0 * sky_rows)
    owner_ids = footprint_owner[0, :, 0]
    tile_rows = footprint_row[0]
    onehot_owner = (owner_ids[:, None] == jnp.arange(n_sky, dtype=jnp.int32)[None, :]).astype(
        jnp.int32
    )
    ranks = jnp.sum((jnp.cumsum(onehot_owner, axis=0) - onehot_owner) * onehot_owner, axis=1)
    slot_of = owner_ids * capacity + ranks
    packing = jnp.arange(slot_count, dtype=jnp.int32)[:, None] == slot_of[None, :]
    requested = jnp.sum(jnp.where(packing, tile_rows[None, :] + 1, 0), axis=1) - 1
    slot_source = jnp.sum(jnp.where(packing, jnp.arange(foot_tiles)[None, :] + 1, 0), axis=1) - 1
    slot_source = jnp.where(slot_source < 0, foot_tiles, slot_source)
    observed = exposures[0]
    tile_weights = weights[0]
    kernel_ids = kernel_index[0]
    incoming = lax.all_to_all(requested, "sky", split_axis=0, concat_axis=0, tiled=True)
    left_kernels, right_kernels = pick_kernels(kernel_ids, kernels)
    receive_map = jnp.arange(sky_rows, dtype=jnp.int32)[:, None] == incoming[None, :]
    local_counts = float(expo_count) * jnp.sum(receive_map.astype(jnp.float32), axis=1)
    receive_half = receive_map.astype(jnp.bfloat16)
    safe_rows = jnp.maximum(incoming, 0)
    rows_per = sky_rows // n_exp
    own_rows = (lax.axis_index("exp_hi") * lax.axis_size("exp_lo") + lax.axis_index("exp_lo")) * rows_per
    count_tile = jnp.broadcast_to(
        local_counts[:, None], (sky_rows, tile_edge)
    )
    sky_now = sky_start
    for iteration in range(ITERS):
        sky_half = sky_now.astype(jnp.bfloat16)
        replies = lax.all_to_all(
            sky_half[safe_rows], "sky", split_axis=0, concat_axis=0, tiled=True
        )
        fetched = replies[slot_of]
        adjoint = adjoint_tiles(fetched, left_kernels, right_kernels, tile_weights, observed)
        padded_adjoint = jnp.concatenate(
            [adjoint, jnp.zeros((1, tile_edge, tile_edge), adjoint.dtype)], axis=0
        )
        outgoing = padded_adjoint[slot_source]
        arrived = lax.all_to_all(outgoing, "sky", split_axis=0, concat_axis=0, tiled=True)
        if iteration == 0:
            count_tiles = lax.all_gather(count_tile, ("exp_hi", "exp_lo"), axis=0, tiled=True)
            count_tiles, arrived = lax.optimization_barrier((count_tiles, arrived))
            counts = jnp.sum(
                count_tiles.astype(jnp.float32).reshape(n_exp, sky_rows, tile_edge)[:, :, 0], axis=0
            )
            denominator = weight_ceiling * counts + 8.0 * prior_weight
            own_denominator = lax.dynamic_slice_in_dim(denominator, own_rows, rows_per)
        partial_value = jnp.einsum(
            "rj,juv->ruv", receive_half, arrived, preferred_element_type=jnp.float32
        )
        payload = partial_value.astype(jnp.bfloat16).reshape(n_exp, rows_per * tile_edge, tile_edge)
        row_parts = lax.all_to_all(
            payload, ("exp_hi", "exp_lo"), split_axis=0, concat_axis=0, tiled=True
        )
        summed = jnp.sum(row_parts.astype(jnp.float32).reshape((n_exp,) + payload.shape[1:]), axis=0)
        own_total = summed[: rows_per * tile_edge].reshape(rows_per, tile_edge, tile_edge)
        scaled = own_total / own_denominator[:, None, None]
        gathered = lax.all_gather(scaled.astype(jnp.bfloat16), "exp_lo", axis=0, tiled=True)
        gathered = lax.all_gather(gathered, "exp_hi", axis=0, tiled=True)
        laplacian = laplace_image(padded_2(sky_now, (("sky", 2),), 1))
        smooth = prior_weight * laplacian / denominator[:, None, None]
        sky_now = sky_now - (gathered.astype(jnp.float32) + smooth)
    return sky_now


def solution(mesh):
    n_exp = mesh.shape["exp"]
    inner = 4 if n_exp % 4 == 0 else 1
    split_mesh = jax.sharding.Mesh(
        mesh.devices.reshape((n_exp // inner, inner) + mesh.devices.shape[1:]),
        ("exp_hi", "exp_lo", "sky"),
    )
    exp_axes = ("exp_hi", "exp_lo")
    in_specs = (
        P(None, None, "sky"),
        P(exp_axes, "sky", None, None, None),
        P(exp_axes, "sky", None),
        P(exp_axes, "sky", None),
        P(exp_axes, "sky"),
        P(exp_axes, "sky", None, None),
        P(),
    )
    out_specs = P(None, None, "sky")
    return jax.shard_map(
        per_device, mesh=split_mesh, in_specs=in_specs, out_specs=out_specs, check_vma=False
    )
```

```python
import jax
import jax.numpy as jnp
from jax import lax
from jax.sharding import PartitionSpec as P

ITERS = 2


weight_ceiling = 2.0


def padded_2(cells, sides, width):
    for axis, dim in sides:
        count = lax.axis_size(axis)
        ends = count - 1
        head = lax.slice_in_dim(cells, 0, width, axis=dim)
        tail = lax.slice_in_dim(cells, cells.shape[dim] - width, cells.shape[dim], axis=dim)
        cells = jnp.concatenate(
            [
                lax.ppermute(tail, axis, [(i, (i + 1) % count) for i in range(ends)]),
                cells,
                lax.ppermute(head, axis, [((i + 1) % count, i) for i in range(ends)]),
            ],
            axis=dim,
        )
    return cells


def pick_kernels(kernel_ids, kernels):
    table_size = kernels.shape[0]
    tile_edge = kernels.shape[1]
    onehot = (kernel_ids[..., None] == jnp.arange(table_size, dtype=jnp.int32)).astype(jnp.bfloat16)
    onehot = onehot.reshape(-1, table_size)
    selected = jnp.dot(onehot, kernels.reshape(table_size, -1), preferred_element_type=jnp.float32)
    selected = selected.astype(jnp.bfloat16).reshape(kernel_ids.shape + (tile_edge, tile_edge))
    return (selected[..., 0, :, :], selected[..., 1, :, :])


def adjoint_tiles(fetched, left_kernels, right_kernels, tile_weights, observed):
    left_product = jnp.einsum(
        "fetu,fuv->fetv", left_kernels, fetched, preferred_element_type=jnp.float32
    ).astype(jnp.bfloat16)
    predicted = jnp.einsum(
        "fetv,fewv->fetw", left_product, right_kernels, preferred_element_type=jnp.float32
    )
    residual = tile_weights.astype(jnp.float32)[..., None, None] * (
        predicted - observed.astype(jnp.float32)
    )
    residual = residual.astype(jnp.bfloat16)
    back_product = jnp.einsum(
        "feut,feuw->fetw", left_kernels, residual, preferred_element_type=jnp.float32
    ).astype(jnp.bfloat16)
    summed = jnp.sum(
        jnp.einsum(
            "fetw,fewv->fetv", back_product, right_kernels, preferred_element_type=jnp.float32
        ),
        axis=1,
    )
    return summed.astype(jnp.bfloat16)


def laplace_image(padded):
    image_rows = padded.reshape(padded.shape[0] * padded.shape[1], padded.shape[2])
    center = image_rows[:, 1:-1]
    vertical = jnp.pad(center, ((1, 1), (0, 0)))
    laplacian = 4.0 * center - image_rows[:, :-2] - image_rows[:, 2:] - vertical[:-2] - vertical[2:]
    return laplacian.reshape(padded.shape[0], padded.shape[1], padded.shape[2] - 2)


def per_device(
    sky_start, exposures, weights, footprint_owner, footprint_row, kernel_index, kernels
):
    sky_rows = sky_start.shape[0]
    tile_edge = sky_start.shape[1]
    foot_tiles = footprint_row.shape[1]
    expo_count = exposures.shape[2]
    n_sky = lax.axis_size("sky")
    n_exp = lax.axis_size("exp")
    capacity = max(2, 3 * foot_tiles // (2 * n_sky))
    slot_count = n_sky * capacity
    prior_weight = n_exp * foot_tiles * expo_count / (8.0 * sky_rows)
    owner_ids = footprint_owner[0, :, 0]
    tile_rows = footprint_row[0]
    onehot_owner = (owner_ids[:, None] == jnp.arange(n_sky, dtype=jnp.int32)[None, :]).astype(
        jnp.int32
    )
    ranks = jnp.sum((jnp.cumsum(onehot_owner, axis=0) - onehot_owner) * onehot_owner, axis=1)
    slot_of = owner_ids * capacity + ranks
    packing = jnp.arange(slot_count, dtype=jnp.int32)[:, None] == slot_of[None, :]
    requested = jnp.sum(jnp.where(packing, tile_rows[None, :] + 1, 0), axis=1) - 1
    observed = exposures[0]
    tile_weights = weights[0]
    kernel_ids = kernel_index[0]
    incoming = lax.all_to_all(requested, "sky", split_axis=0, concat_axis=0, tiled=True)
    left_kernels, right_kernels = pick_kernels(kernel_ids, kernels)
    receive_map = jnp.arange(sky_rows, dtype=jnp.int32)[:, None] == incoming[None, :]
    local_counts = float(expo_count) * jnp.sum(receive_map.astype(jnp.float32), axis=1)
    receive_half = receive_map.astype(jnp.bfloat16)
    packing_half = packing.astype(jnp.bfloat16)
    safe_rows = jnp.maximum(incoming, 0)
    rows_per = sky_rows // n_exp
    own_rows = lax.axis_index("exp") * rows_per
    count_tile = jnp.broadcast_to(
        local_counts[:, None], (sky_rows, tile_edge)
    )
    sky_now = sky_start
    for iteration in range(ITERS):
        sky_half = sky_now.astype(jnp.bfloat16)
        replies = lax.all_to_all(
            sky_half[safe_rows], "sky", split_axis=0, concat_axis=0, tiled=True
        )
        fetched = jnp.einsum(
            "jf,juv->fuv", packing_half, replies, preferred_element_type=jnp.float32
        ).astype(jnp.bfloat16)
        adjoint = adjoint_tiles(fetched, left_kernels, right_kernels, tile_weights, observed)
        outgoing = jnp.einsum(
            "jf,fuv->juv", packing_half, adjoint, preferred_element_type=jnp.float32
        ).astype(jnp.bfloat16)
        arrived = lax.all_to_all(outgoing, "sky", split_axis=0, concat_axis=0, tiled=True)
        if iteration == 0:
            count_tiles = lax.all_gather(count_tile, "exp", axis=0, tiled=True)
            count_tiles, arrived = lax.optimization_barrier((count_tiles, arrived))
            counts = jnp.sum(
                count_tiles.astype(jnp.float32).reshape(n_exp, sky_rows, tile_edge)[:, :, 0], axis=0
            )
            denominator = weight_ceiling * counts + 8.0 * prior_weight
            own_denominator = lax.dynamic_slice_in_dim(denominator, own_rows, rows_per)
        partial_value = jnp.einsum(
            "rj,juv->ruv", receive_half, arrived, preferred_element_type=jnp.float32
        )
        payload = partial_value.astype(jnp.bfloat16).reshape(n_exp, rows_per * tile_edge, tile_edge)
        row_parts = lax.all_to_all(payload, "exp", split_axis=0, concat_axis=0, tiled=True)
        summed = jnp.sum(row_parts.astype(jnp.float32).reshape((n_exp,) + payload.shape[1:]), axis=0)
        own_total = summed[: rows_per * tile_edge].reshape(rows_per, tile_edge, tile_edge)
        scaled = own_total / own_denominator[:, None, None]
        gathered = lax.all_gather(scaled.astype(jnp.bfloat16), "exp", axis=0, tiled=True)
        laplacian = laplace_image(padded_2(sky_now, (("sky", 2),), 1))
        smooth = prior_weight * laplacian / denominator[:, None, None]
        sky_now = sky_now - (gathered.astype(jnp.float32) + smooth)
    return sky_now


def solution(mesh):
    in_specs = (
        P(None, None, "sky"),
        P("exp", "sky", None, None, None),
        P("exp", "sky", None),
        P("exp", "sky", None),
        P("exp", "sky"),
        P("exp", "sky", None, None),
        P(),
    )
    out_specs = P(None, None, "sky")
    return jax.shard_map(
        per_device, mesh=mesh, in_specs=in_specs, out_specs=out_specs, check_vma=False
    )
```

```python
import jax
import jax.numpy as jnp
from jax import lax
from jax.sharding import PartitionSpec as P

ITERS = 2


weight_ceiling = 2.0


def padded_2(cells, sides, width):
    for axis, dim in sides:
        count = lax.axis_size(axis)
        ends = count - 1
        head = lax.slice_in_dim(cells, 0, width, axis=dim)
        tail = lax.slice_in_dim(cells, cells.shape[dim] - width, cells.shape[dim], axis=dim)
        cells = jnp.concatenate(
            [
                lax.ppermute(tail, axis, [(i, (i + 1) % count) for i in range(ends)]),
                cells,
                lax.ppermute(head, axis, [((i + 1) % count, i) for i in range(ends)]),
            ],
            axis=dim,
        )
    return cells


def pick_kernels(kernel_ids, kernels):
    table_size = kernels.shape[0]
    tile_edge = kernels.shape[1]
    onehot = (kernel_ids[..., None] == jnp.arange(table_size, dtype=jnp.int32)).astype(jnp.bfloat16)
    onehot = onehot.reshape(-1, table_size)
    selected = jnp.dot(onehot, kernels.reshape(table_size, -1), preferred_element_type=jnp.float32)
    selected = selected.astype(jnp.bfloat16).reshape(kernel_ids.shape + (tile_edge, tile_edge))
    return (selected[..., 0, :, :], selected[..., 1, :, :])


def adjoint_tiles(fetched, left_kernels, right_kernels, tile_weights, observed):
    left_product = jnp.einsum(
        "fetu,fuv->fetv", left_kernels, fetched, preferred_element_type=jnp.float32
    ).astype(jnp.bfloat16)
    predicted = jnp.einsum(
        "fetv,fewv->fetw", left_product, right_kernels, preferred_element_type=jnp.float32
    )
    residual = tile_weights.astype(jnp.float32)[..., None, None] * (
        predicted - observed.astype(jnp.float32)
    )
    residual = residual.astype(jnp.bfloat16)
    back_product = jnp.einsum(
        "feut,feuw->fetw", left_kernels, residual, preferred_element_type=jnp.float32
    ).astype(jnp.bfloat16)
    summed = jnp.sum(
        jnp.einsum(
            "fetw,fewv->fetv", back_product, right_kernels, preferred_element_type=jnp.float32
        ),
        axis=1,
    )
    return summed.astype(jnp.bfloat16)


def laplace_image(padded):
    image_rows = padded.reshape(padded.shape[0] * padded.shape[1], padded.shape[2])
    center = image_rows[:, 1:-1]
    vertical = jnp.pad(center, ((1, 1), (0, 0)))
    laplacian = 4.0 * center - image_rows[:, :-2] - image_rows[:, 2:] - vertical[:-2] - vertical[2:]
    return laplacian.reshape(padded.shape[0], padded.shape[1], padded.shape[2] - 2)


def per_device(
    sky_start, exposures, weights, footprint_owner, footprint_row, kernel_index, kernels
):
    sky_rows = sky_start.shape[0]
    tile_edge = sky_start.shape[1]
    foot_tiles = footprint_row.shape[1]
    expo_count = exposures.shape[2]
    n_sky = lax.axis_size("sky")
    n_exp = lax.axis_size("exp")
    capacity = max(2, 3 * foot_tiles // (2 * n_sky))
    slot_count = n_sky * capacity
    prior_weight = n_exp * foot_tiles * expo_count / (8.0 * sky_rows)
    owner_ids = footprint_owner[0, :, 0]
    tile_rows = footprint_row[0]
    positions = jnp.arange(foot_tiles, dtype=jnp.int32)
    earlier_same = (owner_ids[:, None] == owner_ids[None, :]) & (
        positions[:, None] > positions[None, :]
    )
    ranks = jnp.sum(earlier_same.astype(jnp.int32), axis=1)
    slot_of = owner_ids * capacity + ranks
    packing = jnp.arange(slot_count, dtype=jnp.int32)[:, None] == slot_of[None, :]
    requested = jnp.sum(jnp.where(packing, tile_rows[None, :] + 1, 0), axis=1) - 1
    slot_source = jnp.sum(jnp.where(packing, jnp.arange(foot_tiles)[None, :] + 1, 0), axis=1) - 1
    slot_source = jnp.where(slot_source < 0, foot_tiles, slot_source)
    observed = exposures[0]
    tile_weights = weights[0]
    kernel_ids = kernel_index[0]
    incoming = lax.all_to_all(requested, "sky", split_axis=0, concat_axis=0, tiled=True)
    left_kernels, right_kernels = pick_kernels(kernel_ids, kernels)
    receive_map = jnp.arange(sky_rows, dtype=jnp.int32)[:, None] == incoming[None, :]
    local_counts = float(expo_count) * jnp.sum(receive_map.astype(jnp.float32), axis=1)
    receive_half = receive_map.astype(jnp.bfloat16)
    safe_rows = jnp.maximum(incoming, 0)
    rows_per = sky_rows // n_exp
    own_rows = lax.axis_index("exp") * rows_per
    count_tile = jnp.broadcast_to(
        local_counts[:, None], (sky_rows, tile_edge)
    )
    sky_now = sky_start
    for iteration in range(ITERS):
        sky_half = sky_now.astype(jnp.bfloat16)
        replies = lax.all_to_all(
            sky_half[safe_rows], "sky", split_axis=0, concat_axis=0, tiled=True
        )
        fetched = replies[slot_of]
        adjoint = adjoint_tiles(fetched, left_kernels, right_kernels, tile_weights, observed)
        padded_adjoint = jnp.concatenate(
            [adjoint, jnp.zeros((1, tile_edge, tile_edge), adjoint.dtype)], axis=0
        )
        outgoing = padded_adjoint[slot_source]
        arrived = lax.all_to_all(outgoing, "sky", split_axis=0, concat_axis=0, tiled=True)
        if iteration == 0:
            count_tiles = lax.all_gather(count_tile, "exp", axis=0, tiled=True)
            count_tiles, arrived = lax.optimization_barrier((count_tiles, arrived))
            counts = jnp.sum(
                count_tiles.astype(jnp.float32).reshape(n_exp, sky_rows, tile_edge)[:, :, 0], axis=0
            )
            denominator = weight_ceiling * counts + 8.0 * prior_weight
            own_denominator = lax.dynamic_slice_in_dim(denominator, own_rows, rows_per)
        partial_value = jnp.einsum(
            "rj,juv->ruv", receive_half, arrived, preferred_element_type=jnp.float32
        )
        payload = partial_value.astype(jnp.bfloat16).reshape(n_exp, rows_per * tile_edge, tile_edge)
        row_parts = lax.all_to_all(payload, "exp", split_axis=0, concat_axis=0, tiled=True)
        summed = jnp.sum(row_parts.astype(jnp.float32).reshape((n_exp,) + payload.shape[1:]), axis=0)
        own_total = summed[: rows_per * tile_edge].reshape(rows_per, tile_edge, tile_edge)
        scaled = own_total / own_denominator[:, None, None]
        gathered = lax.all_gather(scaled.astype(jnp.bfloat16), "exp", axis=0, tiled=True)
        laplacian = laplace_image(padded_2(sky_now, (("sky", 2),), 1))
        smooth = prior_weight * laplacian / denominator[:, None, None]
        sky_now = sky_now - (gathered.astype(jnp.float32) + smooth)
    return sky_now


def solution(mesh):
    in_specs = (
        P(None, None, "sky"),
        P("exp", "sky", None, None, None),
        P("exp", "sky", None),
        P("exp", "sky", None),
        P("exp", "sky"),
        P("exp", "sky", None, None),
        P(),
    )
    out_specs = P(None, None, "sky")
    return jax.shard_map(
        per_device, mesh=mesh, in_specs=in_specs, out_specs=out_specs, check_vma=False
    )
```

```python
import jax
import jax.numpy as jnp
from jax import lax
from jax.sharding import PartitionSpec as P

ITERS = 2


weight_ceiling = 2.0


def padded_2(cells, sides, width):
    for axis, dim in sides:
        count = lax.axis_size(axis)
        ends = count - 1
        head = lax.slice_in_dim(cells, 0, width, axis=dim)
        tail = lax.slice_in_dim(cells, cells.shape[dim] - width, cells.shape[dim], axis=dim)
        cells = jnp.concatenate(
            [
                lax.ppermute(tail, axis, [(i, (i + 1) % count) for i in range(ends)]),
                cells,
                lax.ppermute(head, axis, [((i + 1) % count, i) for i in range(ends)]),
            ],
            axis=dim,
        )
    return cells


def pick_kernels(kernel_ids, kernels):
    table_size = kernels.shape[0]
    tile_edge = kernels.shape[1]
    onehot = (kernel_ids[..., None] == jnp.arange(table_size, dtype=jnp.int32)).astype(jnp.bfloat16)
    onehot = onehot.reshape(-1, table_size)
    selected = jnp.dot(onehot, kernels.reshape(table_size, -1), preferred_element_type=jnp.float32)
    selected = selected.astype(jnp.bfloat16).reshape(kernel_ids.shape + (tile_edge, tile_edge))
    return (selected[..., 0, :, :], selected[..., 1, :, :])


def adjoint_tiles(fetched, left_kernels, right_kernels, tile_weights, observed):
    left_product = jnp.einsum(
        "fetu,fuv->fetv", left_kernels, fetched, preferred_element_type=jnp.float32
    ).astype(jnp.bfloat16)
    predicted = jnp.einsum(
        "fetv,fewv->fetw", left_product, right_kernels, preferred_element_type=jnp.float32
    )
    residual = tile_weights.astype(jnp.float32)[..., None, None] * (
        predicted - observed.astype(jnp.float32)
    )
    residual = residual.astype(jnp.bfloat16)
    back_product = jnp.einsum(
        "feut,feuw->fetw", left_kernels, residual, preferred_element_type=jnp.float32
    ).astype(jnp.bfloat16)
    summed = jnp.sum(
        jnp.einsum(
            "fetw,fewv->fetv", back_product, right_kernels, preferred_element_type=jnp.float32
        ),
        axis=1,
    )
    return summed.astype(jnp.bfloat16)


def laplace_image(padded):
    image_rows = padded.reshape(padded.shape[0] * padded.shape[1], padded.shape[2])
    center = image_rows[:, 1:-1]
    vertical = jnp.pad(center, ((1, 1), (0, 0)))
    laplacian = 4.0 * center - image_rows[:, :-2] - image_rows[:, 2:] - vertical[:-2] - vertical[2:]
    return laplacian.reshape(padded.shape[0], padded.shape[1], padded.shape[2] - 2)


def per_device(
    sky_start, exposures, weights, footprint_owner, footprint_row, kernel_index, kernels
):
    sky_rows = sky_start.shape[0]
    tile_edge = sky_start.shape[1]
    foot_tiles = footprint_row.shape[1]
    expo_count = exposures.shape[2]
    n_sky = lax.axis_size("sky")
    n_exp = lax.axis_size("exp")
    capacity = max(2, 3 * foot_tiles // (2 * n_sky))
    slot_count = n_sky * capacity
    prior_weight = n_exp * foot_tiles * expo_count / (8.0 * sky_rows)
    owner_ids = footprint_owner[0, :, 0]
    tile_rows = footprint_row[0]
    onehot_owner = (owner_ids[:, None] == jnp.arange(n_sky, dtype=jnp.int32)[None, :]).astype(
        jnp.int32
    )
    ranks = jnp.sum((jnp.cumsum(onehot_owner, axis=0) - onehot_owner) * onehot_owner, axis=1)
    slot_of = owner_ids * capacity + ranks
    packing = jnp.arange(slot_count, dtype=jnp.int32)[:, None] == slot_of[None, :]
    requested = jnp.sum(jnp.where(packing, tile_rows[None, :] + 1, 0), axis=1) - 1
    slot_source = jnp.sum(jnp.where(packing, jnp.arange(foot_tiles)[None, :] + 1, 0), axis=1) - 1
    slot_source = jnp.where(slot_source < 0, foot_tiles, slot_source)
    observed = exposures[0]
    tile_weights = weights[0]
    kernel_ids = kernel_index[0]
    incoming = lax.all_to_all(requested, "sky", split_axis=0, concat_axis=0, tiled=True)
    left_kernels, right_kernels = pick_kernels(kernel_ids, kernels)
    receive_map = jnp.arange(sky_rows, dtype=jnp.int32)[:, None] == incoming[None, :]
    local_counts = float(expo_count) * jnp.sum(receive_map.astype(jnp.float32), axis=1)
    receive_half = receive_map.astype(jnp.bfloat16)
    safe_rows = jnp.maximum(incoming, 0)
    rows_per = sky_rows // n_exp
    own_rows = lax.axis_index("exp") * rows_per
    count_tile = jnp.broadcast_to(
        local_counts[:, None], (sky_rows, tile_edge)
    )
    sky_now = sky_start
    for iteration in range(ITERS):
        replies = lax.all_to_all(
            sky_now[safe_rows].astype(jnp.bfloat16), "sky", split_axis=0, concat_axis=0, tiled=True
        )
        fetched = replies[slot_of]
        adjoint = adjoint_tiles(fetched, left_kernels, right_kernels, tile_weights, observed)
        padded_adjoint = jnp.concatenate(
            [adjoint, jnp.zeros((1, tile_edge, tile_edge), adjoint.dtype)], axis=0
        )
        outgoing = padded_adjoint[slot_source]
        arrived = lax.all_to_all(outgoing, "sky", split_axis=0, concat_axis=0, tiled=True)
        if iteration == 0:
            count_tiles = lax.all_gather(count_tile, "exp", axis=0, tiled=True)
            count_tiles, arrived = lax.optimization_barrier((count_tiles, arrived))
            counts = jnp.sum(
                count_tiles.astype(jnp.float32).reshape(n_exp, sky_rows, tile_edge)[:, :, 0], axis=0
            )
            denominator = weight_ceiling * counts + 8.0 * prior_weight
            own_denominator = lax.dynamic_slice_in_dim(denominator, own_rows, rows_per)
        partial_value = jnp.einsum(
            "rj,juv->ruv", receive_half, arrived, preferred_element_type=jnp.float32
        )
        payload = partial_value.astype(jnp.bfloat16).reshape(n_exp, rows_per * tile_edge, tile_edge)
        row_parts = lax.all_to_all(payload, "exp", split_axis=0, concat_axis=0, tiled=True)
        summed = jnp.sum(row_parts.astype(jnp.float32).reshape((n_exp,) + payload.shape[1:]), axis=0)
        own_total = summed[: rows_per * tile_edge].reshape(rows_per, tile_edge, tile_edge)
        scaled = own_total / own_denominator[:, None, None]
        gathered = lax.all_gather(scaled.astype(jnp.bfloat16), "exp", axis=0, tiled=True)
        laplacian = laplace_image(padded_2(sky_now, (("sky", 2),), 1))
        smooth = prior_weight * laplacian / denominator[:, None, None]
        sky_now = sky_now - (gathered.astype(jnp.float32) + smooth)
    return sky_now


def solution(mesh):
    in_specs = (
        P(None, None, "sky"),
        P("exp", "sky", None, None, None),
        P("exp", "sky", None),
        P("exp", "sky", None),
        P("exp", "sky"),
        P("exp", "sky", None, None),
        P(),
    )
    out_specs = P(None, None, "sky")
    return jax.shard_map(
        per_device, mesh=mesh, in_specs=in_specs, out_specs=out_specs, check_vma=False
    )
```

```python
import jax
import jax.numpy as jnp
from jax import lax
from jax.sharding import PartitionSpec as P

ITERS = 2


weight_ceiling = 2.0


def padded_2(cells, sides, width):
    for axis, dim in sides:
        count = lax.axis_size(axis)
        ends = count - 1
        head = lax.slice_in_dim(cells, 0, width, axis=dim)
        tail = lax.slice_in_dim(cells, cells.shape[dim] - width, cells.shape[dim], axis=dim)
        cells = jnp.concatenate(
            [
                lax.ppermute(tail, axis, [(i, (i + 1) % count) for i in range(ends)]),
                cells,
                lax.ppermute(head, axis, [((i + 1) % count, i) for i in range(ends)]),
            ],
            axis=dim,
        )
    return cells


def pick_kernels(kernel_ids, kernels):
    table_size = kernels.shape[0]
    tile_edge = kernels.shape[1]
    onehot = (kernel_ids[..., None] == jnp.arange(table_size, dtype=jnp.int32)).astype(jnp.bfloat16)
    onehot = onehot.reshape(-1, table_size)
    selected = jnp.dot(onehot, kernels.reshape(table_size, -1), preferred_element_type=jnp.float32)
    selected = selected.astype(jnp.bfloat16).reshape(kernel_ids.shape + (tile_edge, tile_edge))
    return (selected[..., 0, :, :], selected[..., 1, :, :])


def adjoint_tiles(fetched, left_kernels, right_kernels, tile_weights, observed):
    left_product = jnp.einsum(
        "fetu,fuv->fetv", left_kernels, fetched, preferred_element_type=jnp.float32
    ).astype(jnp.bfloat16)
    predicted = jnp.einsum(
        "fetv,fewv->fetw", left_product, right_kernels, preferred_element_type=jnp.float32
    )
    residual = tile_weights.astype(jnp.float32)[..., None, None] * (
        predicted - observed.astype(jnp.float32)
    )
    residual = residual.astype(jnp.bfloat16)
    back_product = jnp.einsum(
        "feut,feuw->fetw", left_kernels, residual, preferred_element_type=jnp.float32
    ).astype(jnp.bfloat16)
    summed = jnp.sum(
        jnp.einsum(
            "fetw,fewv->fetv", back_product, right_kernels, preferred_element_type=jnp.float32
        ),
        axis=1,
    )
    return summed.astype(jnp.bfloat16)


def laplace_image(padded):
    image_rows = padded.reshape(padded.shape[0] * padded.shape[1], padded.shape[2])
    center = image_rows[:, 1:-1]
    vertical = jnp.pad(center, ((1, 1), (0, 0)))
    laplacian = 4.0 * center - image_rows[:, :-2] - image_rows[:, 2:] - vertical[:-2] - vertical[2:]
    return laplacian.reshape(padded.shape[0], padded.shape[1], padded.shape[2] - 2)


def per_device(
    sky_start, exposures, weights, footprint_owner, footprint_row, kernel_index, kernels
):
    sky_rows = sky_start.shape[0]
    tile_edge = sky_start.shape[1]
    foot_tiles = footprint_row.shape[1]
    expo_count = exposures.shape[2]
    n_sky = lax.axis_size("sky")
    n_exp = lax.axis_size("exp")
    capacity = max(2, 3 * foot_tiles // (2 * n_sky))
    slot_count = n_sky * capacity
    prior_weight = n_exp * foot_tiles * expo_count / (8.0 * sky_rows)
    owner_ids = footprint_owner[0, :, 0]
    tile_rows = footprint_row[0]
    onehot_owner = (owner_ids[:, None] == jnp.arange(n_sky, dtype=jnp.int32)[None, :]).astype(
        jnp.int32
    )
    ranks = jnp.sum((jnp.cumsum(onehot_owner, axis=0) - onehot_owner) * onehot_owner, axis=1)
    slot_of = owner_ids * capacity + ranks
    packing = jnp.arange(slot_count, dtype=jnp.int32)[:, None] == slot_of[None, :]
    requested = jnp.sum(jnp.where(packing, tile_rows[None, :] + 1, 0), axis=1) - 1
    slot_source = jnp.sum(jnp.where(packing, jnp.arange(foot_tiles)[None, :] + 1, 0), axis=1) - 1
    slot_source = jnp.where(slot_source < 0, foot_tiles, slot_source)
    observed = exposures[0]
    tile_weights = weights[0]
    kernel_ids = kernel_index[0]
    incoming = lax.all_to_all(requested, "sky", split_axis=0, concat_axis=0, tiled=True)
    left_kernels, right_kernels = pick_kernels(kernel_ids, kernels)
    receive_map = jnp.arange(sky_rows, dtype=jnp.int32)[:, None] == incoming[None, :]
    local_counts = float(expo_count) * jnp.sum(receive_map.astype(jnp.float32), axis=1)
    receive_half = receive_map.astype(jnp.bfloat16)
    safe_rows = jnp.maximum(incoming, 0)
    rows_per = sky_rows // n_exp
    own_rows = lax.axis_index("exp") * rows_per
    count_tile = jnp.broadcast_to(
        local_counts[:, None], (sky_rows, tile_edge)
    )
    sky_now = sky_start
    for iteration in range(ITERS):
        replies = lax.all_to_all(
            sky_now[safe_rows].astype(jnp.bfloat16), "sky", split_axis=0, concat_axis=0, tiled=True
        )
        fetched = replies[slot_of]
        adjoint = adjoint_tiles(fetched, left_kernels, right_kernels, tile_weights, observed)
        outgoing = jnp.where(
            (slot_source < foot_tiles)[:, None, None],
            adjoint[jnp.minimum(slot_source, foot_tiles - 1)],
            jnp.zeros((), adjoint.dtype),
        )
        arrived = lax.all_to_all(outgoing, "sky", split_axis=0, concat_axis=0, tiled=True)
        if iteration == 0:
            count_tiles = lax.all_gather(count_tile, "exp", axis=0, tiled=True)
            count_tiles, arrived = lax.optimization_barrier((count_tiles, arrived))
            counts = jnp.sum(
                count_tiles.astype(jnp.float32).reshape(n_exp, sky_rows, tile_edge)[:, :, 0], axis=0
            )
            denominator = weight_ceiling * counts + 8.0 * prior_weight
            own_denominator = lax.dynamic_slice_in_dim(denominator, own_rows, rows_per)
        partial_value = jnp.einsum(
            "rj,juv->ruv", receive_half, arrived, preferred_element_type=jnp.float32
        )
        payload = partial_value.astype(jnp.bfloat16).reshape(n_exp, rows_per * tile_edge, tile_edge)
        row_parts = lax.all_to_all(payload, "exp", split_axis=0, concat_axis=0, tiled=True)
        summed = jnp.sum(row_parts.astype(jnp.float32).reshape((n_exp,) + payload.shape[1:]), axis=0)
        own_total = summed[: rows_per * tile_edge].reshape(rows_per, tile_edge, tile_edge)
        scaled = own_total / own_denominator[:, None, None]
        gathered = lax.all_gather(scaled.astype(jnp.bfloat16), "exp", axis=0, tiled=True)
        laplacian = laplace_image(padded_2(sky_now, (("sky", 2),), 1))
        smooth = prior_weight * laplacian / denominator[:, None, None]
        sky_now = sky_now - (gathered.astype(jnp.float32) + smooth)
    return sky_now


def solution(mesh):
    in_specs = (
        P(None, None, "sky"),
        P("exp", "sky", None, None, None),
        P("exp", "sky", None),
        P("exp", "sky", None),
        P("exp", "sky"),
        P("exp", "sky", None, None),
        P(),
    )
    out_specs = P(None, None, "sky")
    return jax.shard_map(
        per_device, mesh=mesh, in_specs=in_specs, out_specs=out_specs, check_vma=False
    )
```
